32 devices in a mesh: kvh: 2 (over x), seq: 16 (over z, y, core).
Axes of the slice: x: 2, y: 2, z: 4, core: 2. Of those that a mesh axis runs over, the one named last changes fastest.
Arguments:
- queries: bfloat16 [6144, 2048], P('seq', 'kvh'), may hold values from -180 to 180
- own_kv: bfloat16 [6144, 512], P('seq', 'kvh'), may hold values from -7 to 7
- library: bfloat16 [48, 128, 512], P('seq', None, 'kvh'), may hold values from -6 to 6
- fresh_kv: bfloat16 [16, 16, 64, 512], P('seq', None, 'kvh'), may hold values from -6 to 6
- retrieved: int32 [16, 16], P('seq'), may hold values from 0 to 47, as said below
- stretch_slot: int32 [48], replicated, may hold values from 0 to 47, as said below
- stretch_len: int32 [48], replicated, may hold values from 32 to 128
- recompute_pos: int32 [16, 16, 64], P('seq'), may hold values from 0 to 127, as said below
Outputs:
- attended: bfloat16 [6144, 2048], P('seq', 'kvh')
The draws below stay inside these ranges and needn't reach their ends.
Inputs may be any that keep to these rules, and one draw needn't show every extreme that they name: The 16 rows r[c, j] = stretch_slot[retrieved[c, j]] of one context have distinct owners r[c, j] // 3. `stretch_slot`: each library row is named once. `recompute_pos`: position i of a stretch's list lies in [i * 2, (i + 1) * 2).
All inputs are finite; a program needn't handle non-finite values.
Results may differ from the reference program's by a relative error of at most 0.0049.
Values may be sent and summed in bfloat16 or wider, within the bound.
No kernel may reach another device: no remote copies, remote signals or barrier semaphores. Data moves between devices by JAX's collectives and lax.ppermute only.
A program may use at most 64 MiB of HBM per device.

```python
import jax
import jax.numpy as jnp
from jax import lax

HD = 128
GROUP = 8
QR = 384
CL = 128
NCH = 16
NREC = 64
LIB_PER = 3
KVH = 2
CTX = 16
TOKENS = 6144
NLIB = 48
N_SEQ = 16


def own_keys(key):
    base = jnp.clip(jax.random.normal(jax.random.fold_in(key, 11), (TOKENS, KVH, 2 * HD), jnp.float32), -6.0, 6.0)
    return base


def draw_own_kv(key, part):
    return own_keys(key).reshape(TOKENS, KVH * 2 * HD).astype(jnp.bfloat16)


def draw_queries(key, part):
    base = 2.5 * jnp.clip(jax.random.normal(jax.random.fold_in(key, 5), (TOKENS, KVH, GROUP, HD), jnp.float32), -5.0, 5.0)
    return base.reshape(TOKENS, KVH * GROUP * HD).astype(jnp.bfloat16)


def draw_recompute_pos(key, part):
    stride = CL // NREC
    offsets = jax.random.randint(jax.random.fold_in(key, 3), (CTX, NCH, NREC), 0, stride)
    return (jnp.arange(NREC, dtype=jnp.int32) * stride + offsets).astype(jnp.int32)


def slot_table(key):
    return jax.random.permutation(jax.random.fold_in(key, 33), NLIB).astype(jnp.int32)


def wanted_rows(key):
    keys = jax.random.split(jax.random.fold_in(key, 31), CTX)
    owners = jax.vmap(lambda one: jax.random.permutation(one, N_SEQ)[:NCH])(keys).astype(jnp.int32)
    local = jax.random.randint(jax.random.fold_in(key, 32), (CTX, NCH), 0, LIB_PER).astype(jnp.int32)
    return owners * LIB_PER + local


def draw_stretch_slot(key, part):
    return slot_table(key)


def draw_retrieved(key, part):
    inverse = jnp.argsort(slot_table(key), stable=True).astype(jnp.int32)
    return inverse[wanted_rows(key)].astype(jnp.int32)


def with_ends(entries, rng, low, top_value):
    extent = entries.shape
    index_at = [jax.random.randint(jax.random.fold_in(rng, axis), (), 0, extent[axis]) for axis in range(len(extent))]
    entries = entries.at[tuple(index_at)].set(low)
    longest = extent.index(max(extent))
    index_at[longest] = (index_at[longest] + 1) % extent[longest]
    return entries.at[tuple(index_at)].set(top_value)


def steps_of(own_key, extent, cuts, least, top_value):
    gain, own = 1.0, jax.random.fold_in(own_key, 6)
    for axis_at, blocks in cuts:
        heights = jnp.exp(jax.random.uniform(jax.random.fold_in(own, axis_at), (blocks,), jnp.float32, least / len(cuts), top_value / len(cuts)))
        gain = gain * jnp.repeat(heights, extent[axis_at] // blocks).reshape([-1 if axis == axis_at else 1 for axis in range(len(extent))])
    return gain


def normal_values(stream_key, dims, deviation, reach, cuts=(), kind=jnp.bfloat16):
    array = deviation * jax.random.normal(stream_key, dims, jnp.float32)
    if cuts:
        array = array * steps_of(stream_key, dims, cuts, -0.22, 0.18)
    return jnp.clip(array, -reach, reach).astype(kind)


def setup_inputs(seed: int = 0) -> dict:
    key_list = jax.random.split(jax.random.key(seed), 9)
    return {
        "queries": draw_queries(jax.random.fold_in(key_list[8], 71), 0),
        "own_kv": draw_own_kv(jax.random.fold_in(key_list[8], 71), 0),
        "library": normal_values(key_list[2], (NLIB, CL, KVH * 2 * HD), 1.0, 6.0, ((0, 16), (2, 2))),
        "fresh_kv": normal_values(key_list[3], (CTX, NCH, NREC, KVH * 2 * HD), 1.0, 6.0, ((0, 16), (2, 2))),
        "retrieved": draw_retrieved(jax.random.fold_in(key_list[8], 71), 0),
        "stretch_slot": draw_stretch_slot(jax.random.fold_in(key_list[8], 71), 0),
        "stretch_len": with_ends(jax.random.randint(key_list[6], (NLIB,), CL // 4, CL + 1), jax.random.fold_in(key_list[6], 1), CL // 4, CL).astype(jnp.int32),
        "recompute_pos": draw_recompute_pos(jax.random.fold_in(key_list[8], 71), 0),
    }


def reference(queries, own_kv, library, fresh_kv, retrieved, stretch_slot, stretch_len, recompute_pos):
    score_scale = HD ** -0.5
    span = NCH * CL
    column = jnp.arange(span + QR, dtype=jnp.int32)
    row_index = jnp.arange(QR, dtype=jnp.int32)

    def one_context(index):
        row_ids = stretch_slot[retrieved[index]]
        limits = stretch_len[row_ids]
        blocks = library[row_ids]
        stretch_index = jnp.arange(NCH, dtype=jnp.int32)[:, None]
        blocks = blocks.at[stretch_index, recompute_pos[index]].set(fresh_kv[index])
        start = (index * QR).astype(jnp.int32)
        mine = lax.dynamic_slice_in_dim(own_kv, start, QR, 0)
        query_rows = lax.dynamic_slice_in_dim(queries, start, QR, 0)
        all_rows = jnp.concatenate([blocks.reshape(span, KVH, 2 * HD), mine.reshape(QR, KVH, 2 * HD)], 0)
        column_limit = limits[jnp.minimum(column // CL, NCH - 1)]
        visible = jnp.where(column[None, :] < span, (column % CL)[None, :] < column_limit[None, :],
                            (column - span)[None, :] <= row_index[:, None])
        heads = query_rows.reshape(QR, KVH * GROUP, HD)

        def one_head(head):
            query_head = lax.dynamic_index_in_dim(heads, head, 1, keepdims=False)
            head_rows = lax.dynamic_index_in_dim(all_rows, head // GROUP, 1, keepdims=False)
            scores = jnp.dot(query_head, head_rows[:, :HD].T, preferred_element_type=jnp.float32) * score_scale
            scores = jnp.where(visible, scores, -jnp.inf)
            highest = jnp.max(scores, axis=1, keepdims=True)
            expo = jnp.exp(scores - highest)
            weights = (expo / jnp.sum(expo, axis=1, keepdims=True)).astype(jnp.bfloat16)
            return jnp.dot(weights, head_rows[:, HD:], preferred_element_type=jnp.float32).astype(jnp.bfloat16)

        outputs = lax.map(one_head, jnp.arange(KVH * GROUP, dtype=jnp.int32))
        return jnp.transpose(outputs, (1, 0, 2)).reshape(QR, KVH * GROUP * HD)

    everything = lax.map(one_context, jnp.arange(CTX, dtype=jnp.int32))
    return everything.reshape(CTX * QR, KVH * GROUP * HD)
```

```python
import functools

import jax
import jax.numpy as jnp
from jax import lax
from jax.experimental import pallas as pl
from jax.experimental.pallas import tpu as pltpu
from jax.sharding import PartitionSpec as P

HD = 128
CL = 128
TR = 128


def lookup(table, indices):
    hits = indices[..., None] == jnp.arange(table.shape[0], dtype=jnp.int32)
    return jnp.sum(jnp.where(hits, table, 0), axis=-1)


def attend_kernel(owner_ref, bias_ref, pos_ref, recv_ref, fresh_ref, own_ref, q_ref, out_ref, kb_ref, vb_ref):
    nch, nrec = pos_ref.shape
    rows = q_ref.shape[0]
    scale = HD ** (-0.5)

    @pl.when(pl.program_id(0) == 0)
    def _():
        def build(j, carry):
            lib = recv_ref[owner_ref[j]]
            where_at = pos_ref[pl.ds(j, 1), :]
            pick = lax.broadcasted_iota(jnp.int32, (CL, nrec), 0) == where_at
            up = jnp.dot(pick.astype(jnp.bfloat16), fresh_ref[j], preferred_element_type=jnp.float32)
            hit = jnp.max(pick.astype(jnp.float32), axis=1, keepdims=True) > 0
            block = jnp.where(hit, up.astype(jnp.bfloat16), lib)
            at = pl.ds(pl.multiple_of(j * CL, CL), CL)
            kb_ref[at, :] = block[:, :HD]
            vb_ref[at, :] = block[:, HD:]
            return carry

        lax.fori_loop(0, nch, build, 0)

    dims = (((1,), (1,)), ((), ()))
    for t in range(rows // TR):
        qt = q_ref[t * TR:(t + 1) * TR, :]
        s1 = lax.dot_general(qt, kb_ref[...], dims, preferred_element_type=jnp.float32)
        s1 = s1 * scale + bias_ref[...]
        kk = (t + 1) * TR
        s2 = lax.dot_general(qt, own_ref[:kk, :HD], dims, preferred_element_type=jnp.float32) * scale
        row = lax.broadcasted_iota(jnp.int32, (TR, kk), 0) + t * TR
        col = lax.broadcasted_iota(jnp.int32, (TR, kk), 1)
        s2 = jnp.where(col <= row, s2, -jnp.inf)
        top = jnp.maximum(jnp.max(s1, axis=1, keepdims=True), jnp.max(s2, axis=1, keepdims=True))
        e1 = jnp.exp(s1 - top)
        e2 = jnp.exp(s2 - top)
        inv = 1.0 / (jnp.sum(e1, axis=1, keepdims=True) + jnp.sum(e2, axis=1, keepdims=True))
        w1 = (e1 * inv).astype(jnp.bfloat16)
        w2 = (e2 * inv).astype(jnp.bfloat16)
        mixed = jnp.dot(w1, vb_ref[...], preferred_element_type=jnp.float32)
        mixed = mixed + jnp.dot(w2, own_ref[:kk, HD:], preferred_element_type=jnp.float32)
        out_ref[t * TR:(t + 1) * TR, :] = mixed.astype(out_ref.dtype)


def attend(owner, bias, pos, recv, fresh, own_kv, queries):
    rows, width = queries.shape
    heads = width // HD
    nch, nrec = pos.shape
    span = nch * CL
    keys = span + rows
    flops = 4 * heads * rows * keys * HD + 2 * nch * CL * nrec * 2 * HD
    bytes_accessed = 2 * (recv.size + fresh.size + own_kv.size + 2 * queries.size) + 4 * (bias.size + pos.size)

    def full(shape):
        return pl.BlockSpec(shape, lambda g, o: (0,) * len(shape))

    grid_spec = pltpu.PrefetchScalarGridSpec(
        num_scalar_prefetch=1,
        grid=(heads,),
        in_specs=[
            full(bias.shape),
            full(pos.shape),
            full(recv.shape),
            full(fresh.shape),
            full(own_kv.shape),
            pl.BlockSpec((rows, HD), lambda g, o: (0, g)),
        ],
        out_specs=pl.BlockSpec((rows, HD), lambda g, o: (0, g)),
        scratch_shapes=[pltpu.VMEM((span, HD), jnp.bfloat16), pltpu.VMEM((span, HD), jnp.bfloat16)],
    )
    return pl.pallas_call(
        attend_kernel,
        grid_spec=grid_spec,
        out_shape=jax.ShapeDtypeStruct(queries.shape, queries.dtype),
        compiler_params=pltpu.CompilerParams(dimension_semantics=("arbitrary",)),
        cost_estimate=pl.CostEstimate(
            flops=flops, bytes_accessed=bytes_accessed, transcendentals=heads * rows * keys
        ),
    )(owner, bias, pos, recv, fresh, own_kv, queries)


def per_device(
    n_seq, n_kvh, queries, own_kv, library, fresh_kv, retrieved, stretch_slot, stretch_len, recompute_pos
):
    per_owner = library.shape[0]
    wanted = lookup(stretch_slot, retrieved[0])
    owner = wanted // per_owner
    local = wanted % per_owner
    limits = lookup(stretch_len, wanted)

    devices = jnp.arange(n_seq, dtype=jnp.int32)
    request = jnp.sum(jnp.where(owner[None, :] == devices[:, None], local[None, :], 0), axis=1)
    asked = lax.all_to_all(request.reshape(n_seq, 1), "seq", 0, 0, tiled=True).reshape(n_seq)
    send = jnp.broadcast_to(library[0], (n_seq,) + library.shape[1:])
    for k in range(1, per_owner):
        send = jnp.where((asked == k)[:, None, None], library[k], send)
    recv = lax.all_to_all(send, "seq", 0, 0, tiled=True)

    me = lax.axis_index("kvh")
    width = own_kv.shape[1]
    tokens = fresh_kv.shape[2]
    fresh_local = fresh_kv[0]
    pos_local = recompute_pos[0]
    pieces = [lax.dynamic_slice_in_dim(fresh_local, me * width, width, 2)]
    places = [lax.dynamic_slice_in_dim(pos_local, me * tokens, tokens, 1)]
    for shift in range(1, n_kvh):
        target = lax.rem(me + shift, n_kvh)
        piece = lax.dynamic_slice_in_dim(fresh_local, target * width, width, 2)
        pairs = [(i, (i + shift) % n_kvh) for i in range(n_kvh)]
        pieces.append(lax.ppermute(piece, "kvh", pairs))
        source = lax.rem(me + n_kvh - shift, n_kvh)
        places.append(lax.dynamic_slice_in_dim(pos_local, source * tokens, tokens, 1))
    fresh = jnp.concatenate(pieces, 1)
    pos = jnp.concatenate(places, 1)

    column = jnp.arange(CL, dtype=jnp.int32)
    bias = jnp.where(column[None, :] < limits[:, None], 0.0, -jnp.inf).astype(jnp.float32)
    bias = bias.reshape(1, -1)
    return attend(owner, bias, pos, recv, fresh, own_kv, queries)


def solution(mesh):
    placed = (
        P("seq", "kvh"),
        P("seq", "kvh"),
        P("seq", None, "kvh"),
        P("seq", None, "kvh", None),
        P("seq", None),
        P(),
        P(),
        P("seq", None, None),
    )
    body = functools.partial(per_device, mesh.shape["seq"], mesh.shape["kvh"])
    return jax.shard_map(body, mesh=mesh, in_specs=placed, out_specs=P("seq", "kvh"), check_vma=False)
```

```python
import functools

import jax
import jax.numpy as jnp
from jax import lax
from jax.experimental import pallas as pl
from jax.experimental.pallas import tpu as pltpu
from jax.sharding import PartitionSpec as P

HD = 128
CL = 128


def lookup(table, indices):
    hits = indices[..., None] == jnp.arange(table.shape[0], dtype=jnp.int32)
    return jnp.sum(jnp.where(hits, table, 0), axis=-1)


def attend_kernel(
    owner_ref, bias_ref, pos_ref, recv_ref, fresh_ref, own_ref, q_ref, out_ref, kt_ref, vb_ref, ot_ref
):
    nch, nrec = pos_ref.shape
    rows = q_ref.shape[0]
    scale = HD ** (-0.5)

    @pl.when(pl.program_id(0) == 0)
    def _():
        def build(j, carry):
            lib = recv_ref[owner_ref[j]]
            where_at = pos_ref[pl.ds(j, 1), :]
            pick = lax.broadcasted_iota(jnp.int32, (CL, nrec), 0) == where_at
            up = jnp.dot(pick.astype(jnp.bfloat16), fresh_ref[j], preferred_element_type=jnp.float32)
            hit = jnp.max(pick.astype(jnp.float32), axis=1, keepdims=True) > 0
            block = jnp.where(hit, up.astype(jnp.bfloat16), lib)
            at = pl.ds(pl.multiple_of(j * CL, CL), CL)
            kt_ref[:, at] = block[:, :HD].T
            vb_ref[at, :] = block[:, HD:]
            return carry

        lax.fori_loop(0, nch, build, 0)
        ot_ref[...] = own_ref[:, :HD].T

    q = q_ref[...]
    s1 = jnp.dot(q, kt_ref[...], preferred_element_type=jnp.float32) * scale + bias_ref[...]
    s2 = jnp.dot(q, ot_ref[...], preferred_element_type=jnp.float32) * scale
    row = lax.broadcasted_iota(jnp.int32, (rows, rows), 0)
    col = lax.broadcasted_iota(jnp.int32, (rows, rows), 1)
    s2 = jnp.where(col <= row, s2, -jnp.inf)
    top = jnp.maximum(jnp.max(s1, axis=1, keepdims=True), jnp.max(s2, axis=1, keepdims=True))
    e1 = jnp.exp(s1 - top)
    e2 = jnp.exp(s2 - top)
    inv = 1.0 / (jnp.sum(e1, axis=1, keepdims=True) + jnp.sum(e2, axis=1, keepdims=True))
    w1 = (e1 * inv).astype(jnp.bfloat16)
    w2 = (e2 * inv).astype(jnp.bfloat16)
    mixed = jnp.dot(w1, vb_ref[...], preferred_element_type=jnp.float32)
    mixed = mixed + jnp.dot(w2, own_ref[:, HD:], preferred_element_type=jnp.float32)
    out_ref[...] = mixed.astype(out_ref.dtype)


def attend(owner, bias, pos, recv, fresh, own_kv, queries):
    rows, width = queries.shape
    heads = width // HD
    nch, nrec = pos.shape
    span = nch * CL
    keys = span + rows
    flops = 4 * heads * rows * keys * HD + 2 * nch * CL * nrec * 2 * HD
    bytes_accessed = 2 * (recv.size + fresh.size + own_kv.size + 2 * queries.size) + 4 * (bias.size + pos.size)

    def full(shape):
        return pl.BlockSpec(shape, lambda g, o: (0,) * len(shape))

    grid_spec = pltpu.PrefetchScalarGridSpec(
        num_scalar_prefetch=1,
        grid=(heads,),
        in_specs=[
            full(bias.shape),
            full(pos.shape),
            full(recv.shape),
            full(fresh.shape),
            full(own_kv.shape),
            pl.BlockSpec((rows, HD), lambda g, o: (0, g)),
        ],
        out_specs=pl.BlockSpec((rows, HD), lambda g, o: (0, g)),
        scratch_shapes=[
            pltpu.VMEM((HD, span), jnp.bfloat16),
            pltpu.VMEM((span, HD), jnp.bfloat16),
            pltpu.VMEM((HD, rows), jnp.bfloat16),
        ],
    )
    return pl.pallas_call(
        attend_kernel,
        grid_spec=grid_spec,
        out_shape=jax.ShapeDtypeStruct(queries.shape, queries.dtype),
        compiler_params=pltpu.CompilerParams(dimension_semantics=("arbitrary",)),
        cost_estimate=pl.CostEstimate(
            flops=flops, bytes_accessed=bytes_accessed, transcendentals=heads * rows * keys
        ),
    )(owner, bias, pos, recv, fresh, own_kv, queries)


def per_device(
    n_seq, n_kvh, queries, own_kv, library, fresh_kv, retrieved, stretch_slot, stretch_len, recompute_pos
):
    per_owner = library.shape[0]
    wanted = lookup(stretch_slot, retrieved[0])
    owner = wanted // per_owner
    local = wanted % per_owner
    limits = lookup(stretch_len, wanted)

    devices = jnp.arange(n_seq, dtype=jnp.int32)
    request = jnp.sum(jnp.where(owner[None, :] == devices[:, None], local[None, :], 0), axis=1)
    asked = lax.all_to_all(request.reshape(n_seq, 1), "seq", 0, 0, tiled=True).reshape(n_seq)
    send = jnp.broadcast_to(library[0], (n_seq,) + library.shape[1:])
    for k in range(1, per_owner):
        send = jnp.where((asked == k)[:, None, None], library[k], send)
    recv = lax.all_to_all(send, "seq", 0, 0, tiled=True)

    me = lax.axis_index("kvh")
    width = own_kv.shape[1]
    tokens = fresh_kv.shape[2]
    fresh_local = fresh_kv[0]
    pos_local = recompute_pos[0]
    pieces = [lax.dynamic_slice_in_dim(fresh_local, me * width, width, 2)]
    places = [lax.dynamic_slice_in_dim(pos_local, me * tokens, tokens, 1)]
    for shift in range(1, n_kvh):
        target = lax.rem(me + shift, n_kvh)
        piece = lax.dynamic_slice_in_dim(fresh_local, target * width, width, 2)
        pairs = [(i, (i + shift) % n_kvh) for i in range(n_kvh)]
        pieces.append(lax.ppermute(piece, "kvh", pairs))
        source = lax.rem(me + n_kvh - shift, n_kvh)
        places.append(lax.dynamic_slice_in_dim(pos_local, source * tokens, tokens, 1))
    fresh = jnp.concatenate(pieces, 1)
    pos = jnp.concatenate(places, 1)

    column = jnp.arange(CL, dtype=jnp.int32)
    bias = jnp.where(column[None, :] < limits[:, None], 0.0, -jnp.inf).astype(jnp.float32)
    bias = bias.reshape(1, -1)
    return attend(owner, bias, pos, recv, fresh, own_kv, queries)


def solution(mesh):
    placed = (
        P("seq", "kvh"),
        P("seq", "kvh"),
        P("seq", None, "kvh"),
        P("seq", None, "kvh", None),
        P("seq", None),
        P(),
        P(),
        P("seq", None, None),
    )
    body = functools.partial(per_device, mesh.shape["seq"], mesh.shape["kvh"])
    return jax.shard_map(body, mesh=mesh, in_specs=placed, out_specs=P("seq", "kvh"), check_vma=False)
```

```python
import functools

import jax
import jax.numpy as jnp
from jax import lax
from jax.experimental import pallas as pl
from jax.experimental.pallas import tpu as pltpu
from jax.sharding import PartitionSpec as P

HD = 128
CL = 128


def lookup(table, indices):
    hits = indices[..., None] == jnp.arange(table.shape[0], dtype=jnp.int32)
    return jnp.sum(jnp.where(hits, table, 0), axis=-1)


def attend_kernel(
    owner_ref, bias_ref, pos_ref, recv_ref, fresh_ref, own_ref, q_ref, out_ref, kt_ref, vb_ref, ot_ref
):
    nch, nrec = pos_ref.shape
    rows = q_ref.shape[0]
    rate = HD ** (-0.5) * 1.4426950408889634

    @pl.when(pl.program_id(0) == 0)
    def _():
        def build(j, carry):
            lib = recv_ref[owner_ref[j]]
            where_at = pos_ref[pl.ds(j, 1), :]
            pick = lax.broadcasted_iota(jnp.int32, (CL, nrec), 0) == where_at
            up = jnp.dot(pick.astype(jnp.bfloat16), fresh_ref[j], preferred_element_type=jnp.float32)
            hit = jnp.max(pick.astype(jnp.float32), axis=1, keepdims=True) > 0
            block = jnp.where(hit, up.astype(jnp.bfloat16), lib)
            at = pl.ds(pl.multiple_of(j * CL, CL), CL)
            kt_ref[:, at] = block[:, :HD].T
            vb_ref[at, :] = block[:, HD:]
            return carry

        lax.fori_loop(0, nch, build, 0)
        ot_ref[...] = own_ref[:, :HD].T

    q = q_ref[...]
    s1 = jnp.dot(q, kt_ref[...], preferred_element_type=jnp.float32) + bias_ref[...]
    s2 = jnp.dot(q, ot_ref[...], preferred_element_type=jnp.float32)
    row = lax.broadcasted_iota(jnp.int32, (rows, rows), 0)
    col = lax.broadcasted_iota(jnp.int32, (rows, rows), 1)
    s2 = jnp.where(col <= row, s2, -jnp.inf)
    top = jnp.maximum(jnp.max(s1, axis=1, keepdims=True), jnp.max(s2, axis=1, keepdims=True))
    e1 = jnp.exp2((s1 - top) * rate)
    e2 = jnp.exp2((s2 - top) * rate)
    total = jnp.sum(e1, axis=1, keepdims=True) + jnp.sum(e2, axis=1, keepdims=True)
    mixed = jnp.dot(e1.astype(jnp.bfloat16), vb_ref[...], preferred_element_type=jnp.float32)
    mixed = mixed + jnp.dot(e2.astype(jnp.bfloat16), own_ref[:, HD:], preferred_element_type=jnp.float32)
    out_ref[...] = (mixed * (1.0 / total)).astype(out_ref.dtype)


def attend(owner, bias, pos, recv, fresh, own_kv, queries):
    rows, width = queries.shape
    heads = width // HD
    nch, nrec = pos.shape
    span = nch * CL
    keys = span + rows
    flops = 4 * heads * rows * keys * HD + 2 * nch * CL * nrec * 2 * HD
    bytes_accessed = 2 * (recv.size + fresh.size + own_kv.size + 2 * queries.size) + 4 * (bias.size + pos.size)

    def full(shape):
        return pl.BlockSpec(shape, lambda g, o: (0,) * len(shape))

    grid_spec = pltpu.PrefetchScalarGridSpec(
        num_scalar_prefetch=1,
        grid=(heads,),
        in_specs=[
            full(bias.shape),
            full(pos.shape),
            full(recv.shape),
            full(fresh.shape),
            full(own_kv.shape),
            pl.BlockSpec((rows, HD), lambda g, o: (0, g)),
        ],
        out_specs=pl.BlockSpec((rows, HD), lambda g, o: (0, g)),
        scratch_shapes=[
            pltpu.VMEM((HD, span), jnp.bfloat16),
            pltpu.VMEM((span, HD), jnp.bfloat16),
            pltpu.VMEM((HD, rows), jnp.bfloat16),
        ],
    )
    return pl.pallas_call(
        attend_kernel,
        grid_spec=grid_spec,
        out_shape=jax.ShapeDtypeStruct(queries.shape, queries.dtype),
        compiler_params=pltpu.CompilerParams(dimension_semantics=("arbitrary",)),
        cost_estimate=pl.CostEstimate(
            flops=flops, bytes_accessed=bytes_accessed, transcendentals=heads * rows * keys
        ),
    )(owner, bias, pos, recv, fresh, own_kv, queries)


def per_device(
    n_seq, n_kvh, queries, own_kv, library, fresh_kv, retrieved, stretch_slot, stretch_len, recompute_pos
):
    per_owner = library.shape[0]
    wanted = lookup(stretch_slot, retrieved[0])
    owner = wanted // per_owner
    local = wanted % per_owner
    limits = lookup(stretch_len, wanted)

    devices = jnp.arange(n_seq, dtype=jnp.int32)
    request = jnp.sum(jnp.where(owner[None, :] == devices[:, None], local[None, :], 0), axis=1)
    asked = lax.all_to_all(request.reshape(n_seq, 1), "seq", 0, 0, tiled=True).reshape(n_seq)
    send = jnp.broadcast_to(library[0], (n_seq,) + library.shape[1:])
    for k in range(1, per_owner):
        send = jnp.where((asked == k)[:, None, None], library[k], send)
    recv = lax.all_to_all(send, "seq", 0, 0, tiled=True)

    me = lax.axis_index("kvh")
    width = own_kv.shape[1]
    tokens = fresh_kv.shape[2]
    fresh_local = fresh_kv[0]
    pos_local = recompute_pos[0]
    pieces = [lax.dynamic_slice_in_dim(fresh_local, me * width, width, 2)]
    places = [lax.dynamic_slice_in_dim(pos_local, me * tokens, tokens, 1)]
    for shift in range(1, n_kvh):
        target = lax.rem(me + shift, n_kvh)
        piece = lax.dynamic_slice_in_dim(fresh_local, target * width, width, 2)
        pairs = [(i, (i + shift) % n_kvh) for i in range(n_kvh)]
        pieces.append(lax.ppermute(piece, "kvh", pairs))
        source = lax.rem(me + n_kvh - shift, n_kvh)
        places.append(lax.dynamic_slice_in_dim(pos_local, source * tokens, tokens, 1))
    fresh = jnp.concatenate(pieces, 1)
    pos = jnp.concatenate(places, 1)

    column = jnp.arange(CL, dtype=jnp.int32)
    bias = jnp.where(column[None, :] < limits[:, None], 0.0, -jnp.inf).astype(jnp.float32)
    bias = bias.reshape(1, -1)
    return attend(owner, bias, pos, recv, fresh, own_kv, queries)


def solution(mesh):
    placed = (
        P("seq", "kvh"),
        P("seq", "kvh"),
        P("seq", None, "kvh"),
        P("seq", None, "kvh", None),
        P("seq", None),
        P(),
        P(),
        P("seq", None, None),
    )
    body = functools.partial(per_device, mesh.shape["seq"], mesh.shape["kvh"])
    return jax.shard_map(body, mesh=mesh, in_specs=placed, out_specs=P("seq", "kvh"), check_vma=False)
```

```python
import functools

import jax
import jax.numpy as jnp
from jax import lax
from jax.experimental import pallas as pl
from jax.experimental.pallas import tpu as pltpu
from jax.sharding import PartitionSpec as P

HD = 128
CL = 128
TR = 128
PAIR = 4


def lookup(table, indices):
    hits = indices[..., None] == jnp.arange(table.shape[0], dtype=jnp.int32)
    return jnp.sum(jnp.where(hits, table, 0), axis=-1)


def attend_kernel(
    owner_ref, bias_ref, pos_ref, recv_ref, fresh_ref, own_ref, q_ref, out_ref, kt_ref, vb_ref, ot_ref
):
    nch, nrec = pos_ref.shape
    rows = q_ref.shape[0]
    rate = HD ** (-0.5) * 1.4426950408889634

    @pl.when(pl.program_id(0) == 0)
    def _():
        def build(j, carry):
            lib = recv_ref[owner_ref[j]]
            where_at = pos_ref[pl.ds(j, 1), :]
            pick = lax.broadcasted_iota(jnp.int32, (CL, nrec), 0) == where_at
            up = jnp.dot(pick.astype(jnp.bfloat16), fresh_ref[j], preferred_element_type=jnp.float32)
            hit = jnp.max(pick.astype(jnp.float32), axis=1, keepdims=True) > 0
            block = jnp.where(hit, up.astype(jnp.bfloat16), lib)
            at = pl.ds(pl.multiple_of(j * CL, CL), CL)
            kt_ref[:, at] = block[:, :HD].T
            vb_ref[at, :] = block[:, HD:]
            return carry

        lax.fori_loop(0, nch, build, 0)
        ot_ref[...] = own_ref[:, :HD].T

    for g in range(q_ref.shape[1] // HD):
        for t in range(rows // TR):
            qt = q_ref[t * TR:(t + 1) * TR, g * HD:(g + 1) * HD]
            s1 = jnp.dot(qt, kt_ref[...], preferred_element_type=jnp.float32) + bias_ref[...]
            kk = (t + 1) * TR
            s2 = jnp.dot(qt, ot_ref[:, :kk], preferred_element_type=jnp.float32)
            row = lax.broadcasted_iota(jnp.int32, (TR, kk), 0) + t * TR
            col = lax.broadcasted_iota(jnp.int32, (TR, kk), 1)
            s2 = jnp.where(col <= row, s2, -jnp.inf)
            top = jnp.maximum(jnp.max(s1, axis=1, keepdims=True), jnp.max(s2, axis=1, keepdims=True))
            e1 = jnp.exp2((s1 - top) * rate)
            e2 = jnp.exp2((s2 - top) * rate)
            inv = 1.0 / (jnp.sum(e1, axis=1, keepdims=True) + jnp.sum(e2, axis=1, keepdims=True))
            w1 = (e1 * inv).astype(jnp.bfloat16)
            w2 = (e2 * inv).astype(jnp.bfloat16)
            mixed = jnp.dot(w1, vb_ref[...], preferred_element_type=jnp.float32)
            mixed = mixed + jnp.dot(w2, own_ref[:kk, HD:], preferred_element_type=jnp.float32)
            out_ref[t * TR:(t + 1) * TR, g * HD:(g + 1) * HD] = mixed.astype(out_ref.dtype)


def attend(owner, bias, pos, recv, fresh, own_kv, queries):
    rows, width = queries.shape
    heads = width // HD
    step = PAIR if heads % PAIR == 0 else 1
    nch, nrec = pos.shape
    span = nch * CL
    keys = span + rows
    flops = 4 * heads * rows * keys * HD + 2 * nch * CL * nrec * 2 * HD
    bytes_accessed = 2 * (recv.size + fresh.size + own_kv.size + 2 * queries.size) + 4 * (bias.size + pos.size)

    def full(shape):
        return pl.BlockSpec(shape, lambda g, o: (0,) * len(shape))

    grid_spec = pltpu.PrefetchScalarGridSpec(
        num_scalar_prefetch=1,
        grid=(heads // step,),
        in_specs=[
            full(bias.shape),
            full(pos.shape),
            full(recv.shape),
            full(fresh.shape),
            full(own_kv.shape),
            pl.BlockSpec((rows, step * HD), lambda g, o: (0, g)),
        ],
        out_specs=pl.BlockSpec((rows, step * HD), lambda g, o: (0, g)),
        scratch_shapes=[
            pltpu.VMEM((HD, span), jnp.bfloat16),
            pltpu.VMEM((span, HD), jnp.bfloat16),
            pltpu.VMEM((HD, rows), jnp.bfloat16),
        ],
    )
    return pl.pallas_call(
        attend_kernel,
        grid_spec=grid_spec,
        out_shape=jax.ShapeDtypeStruct(queries.shape, queries.dtype),
        compiler_params=pltpu.CompilerParams(dimension_semantics=("arbitrary",)),
        cost_estimate=pl.CostEstimate(
            flops=flops, bytes_accessed=bytes_accessed, transcendentals=heads * rows * keys
        ),
    )(owner, bias, pos, recv, fresh, own_kv, queries)


def per_device(
    n_seq, n_kvh, queries, own_kv, library, fresh_kv, retrieved, stretch_slot, stretch_len, recompute_pos
):
    per_owner = library.shape[0]
    wanted = lookup(stretch_slot, retrieved[0])
    owner = wanted // per_owner
    local = wanted % per_owner
    limits = lookup(stretch_len, wanted)

    devices = jnp.arange(n_seq, dtype=jnp.int32)
    request = jnp.sum(jnp.where(owner[None, :] == devices[:, None], local[None, :], 0), axis=1)
    asked = lax.all_to_all(request.reshape(n_seq, 1), "seq", 0, 0, tiled=True).reshape(n_seq)
    send = jnp.broadcast_to(library[0], (n_seq,) + library.shape[1:])
    for k in range(1, per_owner):
        send = jnp.where((asked == k)[:, None, None], library[k], send)
    recv = lax.all_to_all(send, "seq", 0, 0, tiled=True)

    me = lax.axis_index("kvh")
    width = own_kv.shape[1]
    tokens = fresh_kv.shape[2]
    fresh_local = fresh_kv[0]
    pos_local = recompute_pos[0]
    pieces = [lax.dynamic_slice_in_dim(fresh_local, me * width, width, 2)]
    places = [lax.dynamic_slice_in_dim(pos_local, me * tokens, tokens, 1)]
    for shift in range(1, n_kvh):
        target = lax.rem(me + shift, n_kvh)
        piece = lax.dynamic_slice_in_dim(fresh_local, target * width, width, 2)
        pairs = [(i, (i + shift) % n_kvh) for i in range(n_kvh)]
        pieces.append(lax.ppermute(piece, "kvh", pairs))
        source = lax.rem(me + n_kvh - shift, n_kvh)
        places.append(lax.dynamic_slice_in_dim(pos_local, source * tokens, tokens, 1))
    fresh = jnp.concatenate(pieces, 1)
    pos = jnp.concatenate(places, 1)

    column = jnp.arange(CL, dtype=jnp.int32)
    bias = jnp.where(column[None, :] < limits[:, None], 0.0, -jnp.inf).astype(jnp.float32)
    bias = bias.reshape(1, -1)
    return attend(owner, bias, pos, recv, fresh, own_kv, queries)


def solution(mesh):
    placed = (
        P("seq", "kvh"),
        P("seq", "kvh"),
        P("seq", None, "kvh"),
        P("seq", None, "kvh", None),
        P("seq", None),
        P(),
        P(),
        P("seq", None, None),
    )
    body = functools.partial(per_device, mesh.shape["seq"], mesh.shape["kvh"])
    return jax.shard_map(body, mesh=mesh, in_specs=placed, out_specs=P("seq", "kvh"), check_vma=False)
```

```python
import functools

import jax
import jax.numpy as jnp
from jax import lax
from jax.experimental import pallas as pl
from jax.experimental.pallas import tpu as pltpu
from jax.sharding import PartitionSpec as P

HD = 128
CL = 128
TR = 128
PAIR = 4


def lookup(table, indices):
    hits = indices[..., None] == jnp.arange(table.shape[0], dtype=jnp.int32)
    return jnp.sum(jnp.where(hits, table, 0), axis=-1)


def attend_kernel(owner_ref, bias_ref, recv_ref, fresh_ref, own_ref, q_ref, out_ref, kt_ref, vb_ref, ot_ref):
    nch = fresh_ref.shape[0]
    rows = q_ref.shape[0]
    rate = HD ** (-0.5) * 1.4426950408889634

    @pl.when(pl.program_id(0) == 0)
    def _():
        def build(j, carry):
            block = jnp.concatenate([recv_ref[owner_ref[j]], fresh_ref[j]], axis=0)
            at = pl.ds(pl.multiple_of(j * CL, CL), CL)
            kt_ref[:, at] = block[:, :HD].T
            vb_ref[at, :] = block[:, HD:]
            return carry

        lax.fori_loop(0, nch, build, 0)
        ot_ref[...] = own_ref[:, :HD].T

    for g in range(q_ref.shape[1] // HD):
        for t in range(rows // TR):
            qt = q_ref[t * TR:(t + 1) * TR, g * HD:(g + 1) * HD]
            s1 = jnp.dot(qt, kt_ref[...], preferred_element_type=jnp.float32) + bias_ref[...]
            kk = (t + 1) * TR
            s2 = jnp.dot(qt, ot_ref[:, :kk], preferred_element_type=jnp.float32)
            row = lax.broadcasted_iota(jnp.int32, (TR, kk), 0) + t * TR
            col = lax.broadcasted_iota(jnp.int32, (TR, kk), 1)
            s2 = jnp.where(col <= row, s2, -jnp.inf)
            top = jnp.maximum(jnp.max(s1, axis=1, keepdims=True), jnp.max(s2, axis=1, keepdims=True))
            e1 = jnp.exp2((s1 - top) * rate)
            e2 = jnp.exp2((s2 - top) * rate)
            inv = 1.0 / (jnp.sum(e1, axis=1, keepdims=True) + jnp.sum(e2, axis=1, keepdims=True))
            w1 = (e1 * inv).astype(jnp.bfloat16)
            w2 = (e2 * inv).astype(jnp.bfloat16)
            mixed = jnp.dot(w1, vb_ref[...], preferred_element_type=jnp.float32)
            mixed = mixed + jnp.dot(w2, own_ref[:kk, HD:], preferred_element_type=jnp.float32)
            out_ref[t * TR:(t + 1) * TR, g * HD:(g + 1) * HD] = mixed.astype(out_ref.dtype)


def attend(owner, bias, recv, fresh, own_kv, queries):
    rows, width = queries.shape
    heads = width // HD
    step = PAIR if heads % PAIR == 0 else 1
    nch = fresh.shape[0]
    span = nch * CL
    keys = span + rows
    flops = 4 * heads * rows * keys * HD
    bytes_accessed = 2 * (recv.size + fresh.size + own_kv.size + 2 * queries.size) + 4 * bias.size

    def full(shape):
        return pl.BlockSpec(shape, lambda g, o: (0,) * len(shape))

    grid_spec = pltpu.PrefetchScalarGridSpec(
        num_scalar_prefetch=1,
        grid=(heads // step,),
        in_specs=[
            full(bias.shape),
            full(recv.shape),
            full(fresh.shape),
            full(own_kv.shape),
            pl.BlockSpec((rows, step * HD), lambda g, o: (0, g)),
        ],
        out_specs=pl.BlockSpec((rows, step * HD), lambda g, o: (0, g)),
        scratch_shapes=[
            pltpu.VMEM((HD, span), jnp.bfloat16),
            pltpu.VMEM((span, HD), jnp.bfloat16),
            pltpu.VMEM((HD, rows), jnp.bfloat16),
        ],
    )
    return pl.pallas_call(
        attend_kernel,
        grid_spec=grid_spec,
        out_shape=jax.ShapeDtypeStruct(queries.shape, queries.dtype),
        compiler_params=pltpu.CompilerParams(dimension_semantics=("arbitrary",)),
        cost_estimate=pl.CostEstimate(
            flops=flops, bytes_accessed=bytes_accessed, transcendentals=heads * rows * keys
        ),
    )(owner, bias, recv, fresh, own_kv, queries)


def per_device(
    n_seq, n_kvh, queries, own_kv, library, fresh_kv, retrieved, stretch_slot, stretch_len, recompute_pos
):
    per_owner = library.shape[0]
    wanted = lookup(stretch_slot, retrieved[0])
    owner = wanted // per_owner
    local = wanted % per_owner
    limits = lookup(stretch_len, wanted)

    pos_local = recompute_pos[0]
    pair = jnp.arange(pos_local.shape[1], dtype=jnp.int32)
    odd_taken = pos_local - 2 * pair[None, :]
    payload = jnp.concatenate([local[:, None], odd_taken], 1)
    devices = jnp.arange(n_seq, dtype=jnp.int32)
    hits = owner[None, :, None] == devices[:, None, None]
    request = jnp.sum(jnp.where(hits, payload[None], 0), axis=1)
    asked = lax.all_to_all(request, "seq", 0, 0, tiled=True)
    which = asked[:, :1, None]
    odd_given = asked[:, 1:, None]
    halves = library.reshape(per_owner, -1, 2, library.shape[2])
    send = None
    for k in range(per_owner):
        kept = jnp.where(odd_given == 0, halves[k, :, 1][None], halves[k, :, 0][None])
        send = kept if send is None else jnp.where(which == k, kept, send)
    recv = lax.all_to_all(send, "seq", 0, 0, tiled=True)

    me = lax.axis_index("kvh")
    width = own_kv.shape[1]
    tokens = fresh_kv.shape[2]
    fresh_local = fresh_kv[0]
    pieces = [lax.dynamic_slice_in_dim(fresh_local, me * width, width, 2)]
    places = [lax.dynamic_slice_in_dim(pos_local, me * tokens, tokens, 1)]
    for shift in range(1, n_kvh):
        target = lax.rem(me + shift, n_kvh)
        piece = lax.dynamic_slice_in_dim(fresh_local, target * width, width, 2)
        pairs = [(i, (i + shift) % n_kvh) for i in range(n_kvh)]
        pieces.append(lax.ppermute(piece, "kvh", pairs))
        source = lax.rem(me + n_kvh - shift, n_kvh)
        places.append(lax.dynamic_slice_in_dim(pos_local, source * tokens, tokens, 1))
    fresh = jnp.concatenate(pieces, 1)
    pos = jnp.concatenate(places, 1)

    kept_at = 2 * pair[None, :] + 1 - odd_taken
    at = jnp.concatenate([kept_at, pos], 1)
    bias = jnp.where(at < limits[:, None], 0.0, -jnp.inf).astype(jnp.float32)
    bias = bias.reshape(1, -1)
    return attend(owner, bias, recv, fresh, own_kv, queries)


def solution(mesh):
    placed = (
        P("seq", "kvh"),
        P("seq", "kvh"),
        P("seq", None, "kvh"),
        P("seq", None, "kvh", None),
        P("seq", None),
        P(),
        P(),
        P("seq", None, None),
    )
    body = functools.partial(per_device, mesh.shape["seq"], mesh.shape["kvh"])
    return jax.shard_map(body, mesh=mesh, in_specs=placed, out_specs=P("seq", "kvh"), check_vma=False)
```

```python
import functools

import jax
import jax.numpy as jnp
from jax import lax
from jax.experimental import pallas as pl
from jax.experimental.pallas import tpu as pltpu
from jax.sharding import PartitionSpec as P

HD = 128
CL = 128
TR = 128
PAIR = 4


def lookup(table, indices):
    hits = indices[..., None] == jnp.arange(table.shape[0], dtype=jnp.int32)
    return jnp.sum(jnp.where(hits, table, 0), axis=-1)


def attend_kernel(owner_ref, bias_ref, recv_ref, fresh_ref, own_ref, q_ref, out_ref, kt_ref, vb_ref, ot_ref):
    nch = fresh_ref.shape[0]
    rows = q_ref.shape[0]
    rate = HD ** (-0.5) * 1.4426950408889634

    @pl.when(pl.program_id(0) == 0)
    def _():
        def build(j, carry):
            block = jnp.concatenate([recv_ref[owner_ref[j]], fresh_ref[j]], axis=0)
            at = pl.ds(pl.multiple_of(j * CL, CL), CL)
            kt_ref[:, at] = block[:, :HD].T
            vb_ref[at, :] = block[:, HD:]
            return carry

        lax.fori_loop(0, nch, build, 0)
        ot_ref[...] = own_ref[:, :HD].T

    def scores(g, t):
        qt = q_ref[t * TR:(t + 1) * TR, g * HD:(g + 1) * HD]
        s1 = jnp.dot(qt, kt_ref[...], preferred_element_type=jnp.float32) + bias_ref[...]
        kk = (t + 1) * TR
        s2 = jnp.dot(qt, ot_ref[:, :kk], preferred_element_type=jnp.float32)
        row = lax.broadcasted_iota(jnp.int32, (TR, kk), 0) + t * TR
        col = lax.broadcasted_iota(jnp.int32, (TR, kk), 1)
        return s1, jnp.where(col <= row, s2, -jnp.inf)

    def finish(g, t, s1, s2):
        kk = (t + 1) * TR
        top = jnp.maximum(jnp.max(s1, axis=1, keepdims=True), jnp.max(s2, axis=1, keepdims=True))
        e1 = jnp.exp2((s1 - top) * rate)
        e2 = jnp.exp2((s2 - top) * rate)
        inv = 1.0 / (jnp.sum(e1, axis=1, keepdims=True) + jnp.sum(e2, axis=1, keepdims=True))
        w1 = (e1 * inv).astype(jnp.bfloat16)
        w2 = (e2 * inv).astype(jnp.bfloat16)
        mixed = jnp.dot(w1, vb_ref[...], preferred_element_type=jnp.float32)
        mixed = mixed + jnp.dot(w2, own_ref[:kk, HD:], preferred_element_type=jnp.float32)
        out_ref[t * TR:(t + 1) * TR, g * HD:(g + 1) * HD] = mixed.astype(out_ref.dtype)

    tiles = [(g, t) for g in range(q_ref.shape[1] // HD) for t in range(rows // TR)]
    ahead = scores(*tiles[0])
    for k, tile in enumerate(tiles):
        now = ahead
        if k + 1 < len(tiles):
            ahead = scores(*tiles[k + 1])
        finish(*tile, *now)


def attend(owner, bias, recv, fresh, own_kv, queries):
    rows, width = queries.shape
    heads = width // HD
    step = PAIR if heads % PAIR == 0 else 1
    nch = fresh.shape[0]
    span = nch * CL
    keys = span + rows
    flops = 4 * heads * rows * keys * HD
    bytes_accessed = 2 * (recv.size + fresh.size + own_kv.size + 2 * queries.size) + 4 * bias.size

    def full(shape):
        return pl.BlockSpec(shape, lambda g, o: (0,) * len(shape))

    grid_spec = pltpu.PrefetchScalarGridSpec(
        num_scalar_prefetch=1,
        grid=(heads // step,),
        in_specs=[
            full(bias.shape),
            full(recv.shape),
            full(fresh.shape),
            full(own_kv.shape),
            pl.BlockSpec((rows, step * HD), lambda g, o: (0, g)),
        ],
        out_specs=pl.BlockSpec((rows, step * HD), lambda g, o: (0, g)),
        scratch_shapes=[
            pltpu.VMEM((HD, span), jnp.bfloat16),
            pltpu.VMEM((span, HD), jnp.bfloat16),
            pltpu.VMEM((HD, rows), jnp.bfloat16),
        ],
    )
    return pl.pallas_call(
        attend_kernel,
        grid_spec=grid_spec,
        out_shape=jax.ShapeDtypeStruct(queries.shape, queries.dtype),
        compiler_params=pltpu.CompilerParams(dimension_semantics=("arbitrary",)),
        cost_estimate=pl.CostEstimate(
            flops=flops, bytes_accessed=bytes_accessed, transcendentals=heads * rows * keys
        ),
    )(owner, bias, recv, fresh, own_kv, queries)


def per_device(
    n_seq, n_kvh, queries, own_kv, library, fresh_kv, retrieved, stretch_slot, stretch_len, recompute_pos
):
    per_owner = library.shape[0]
    wanted = lookup(stretch_slot, retrieved[0])
    owner = wanted // per_owner
    local = wanted % per_owner
    limits = lookup(stretch_len, wanted)

    pos_local = recompute_pos[0]
    pair = jnp.arange(pos_local.shape[1], dtype=jnp.int32)
    odd_taken = pos_local - 2 * pair[None, :]
    payload = jnp.concatenate([local[:, None], odd_taken], 1)
    devices = jnp.arange(n_seq, dtype=jnp.int32)
    hits = owner[None, :, None] == devices[:, None, None]
    request = jnp.sum(jnp.where(hits, payload[None], 0), axis=1)
    asked = lax.all_to_all(request, "seq", 0, 0, tiled=True)
    which = asked[:, :1, None]
    odd_given = asked[:, 1:, None]
    halves = library.reshape(per_owner, -1, 2, library.shape[2])
    send = None
    for k in range(per_owner):
        kept = jnp.where(odd_given == 0, halves[k, :, 1][None], halves[k, :, 0][None])
        send = kept if send is None else jnp.where(which == k, kept, send)
    recv = lax.all_to_all(send, "seq", 0, 0, tiled=True)

    me = lax.axis_index("kvh")
    width = own_kv.shape[1]
    tokens = fresh_kv.shape[2]
    fresh_local = fresh_kv[0]
    pieces = [lax.dynamic_slice_in_dim(fresh_local, me * width, width, 2)]
    places = [lax.dynamic_slice_in_dim(pos_local, me * tokens, tokens, 1)]
    for shift in range(1, n_kvh):
        target = lax.rem(me + shift, n_kvh)
        piece = lax.dynamic_slice_in_dim(fresh_local, target * width, width, 2)
        pairs = [(i, (i + shift) % n_kvh) for i in range(n_kvh)]
        pieces.append(lax.ppermute(piece, "kvh", pairs))
        source = lax.rem(me + n_kvh - shift, n_kvh)
        places.append(lax.dynamic_slice_in_dim(pos_local, source * tokens, tokens, 1))
    fresh = jnp.concatenate(pieces, 1)
    pos = jnp.concatenate(places, 1)

    kept_at = 2 * pair[None, :] + 1 - odd_taken
    at = jnp.concatenate([kept_at, pos], 1)
    bias = jnp.where(at < limits[:, None], 0.0, -jnp.inf).astype(jnp.float32)
    bias = bias.reshape(1, -1)
    return attend(owner, bias, recv, fresh, own_kv, queries)


def solution(mesh):
    placed = (
        P("seq", "kvh"),
        P("seq", "kvh"),
        P("seq", None, "kvh"),
        P("seq", None, "kvh", None),
        P("seq", None),
        P(),
        P(),
        P("seq", None, None),
    )
    body = functools.partial(per_device, mesh.shape["seq"], mesh.shape["kvh"])
    return jax.shard_map(body, mesh=mesh, in_specs=placed, out_specs=P("seq", "kvh"), check_vma=False)
```

```python
import functools

import jax
import jax.numpy as jnp
from jax import lax
from jax.experimental import pallas as pl
from jax.experimental.pallas import tpu as pltpu
from jax.sharding import PartitionSpec as P

HD = 128
CL = 128
TR = 128
PAIR = 4
LEAD = 2


def lookup(table, indices):
    hits = indices[..., None] == jnp.arange(table.shape[0], dtype=jnp.int32)
    return jnp.sum(jnp.where(hits, table, 0), axis=-1)


def attend_kernel(bias_ref, kept_ref, fresh_ref, own_ref, q_ref, out_ref):
    rows = q_ref.shape[0]
    rate = HD ** (-0.5) * 1.4426950408889634
    nt = (((1,), (1,)), ((), ()))

    def scores(g, t):
        qt = q_ref[t * TR:(t + 1) * TR, g * HD:(g + 1) * HD]
        sk = lax.dot_general(qt, kept_ref[:, :HD], nt, preferred_element_type=jnp.float32)
        sf = lax.dot_general(qt, fresh_ref[:, :HD], nt, preferred_element_type=jnp.float32)
        s1 = jnp.concatenate([sk, sf], 1) + bias_ref[...]
        kk = (t + 1) * TR
        s2 = lax.dot_general(qt, own_ref[:kk, :HD], nt, preferred_element_type=jnp.float32)
        row = lax.broadcasted_iota(jnp.int32, (TR, kk), 0) + t * TR
        col = lax.broadcasted_iota(jnp.int32, (TR, kk), 1)
        return s1, jnp.where(col <= row, s2, -jnp.inf)

    def finish(g, t, s1, s2):
        kk = (t + 1) * TR
        top = jnp.maximum(jnp.max(s1, axis=1, keepdims=True), jnp.max(s2, axis=1, keepdims=True))
        e1 = jnp.exp2((s1 - top) * rate)
        e2 = jnp.exp2((s2 - top) * rate)
        inv = 1.0 / (jnp.sum(e1, axis=1, keepdims=True) + jnp.sum(e2, axis=1, keepdims=True))
        w1 = (e1 * inv).astype(jnp.bfloat16)
        w2 = (e2 * inv).astype(jnp.bfloat16)
        split = kept_ref.shape[0]
        mixed = jnp.dot(w1[:, :split], kept_ref[:, HD:], preferred_element_type=jnp.float32)
        mixed = mixed + jnp.dot(w1[:, split:], fresh_ref[:, HD:], preferred_element_type=jnp.float32)
        mixed = mixed + jnp.dot(w2, own_ref[:kk, HD:], preferred_element_type=jnp.float32)
        out_ref[t * TR:(t + 1) * TR, g * HD:(g + 1) * HD] = mixed.astype(out_ref.dtype)

    tiles = [(g, t) for g in range(q_ref.shape[1] // HD) for t in range(rows // TR)]
    ready = [scores(*tile) for tile in tiles[:LEAD]]
    for k, tile in enumerate(tiles):
        if k + LEAD < len(tiles):
            ready.append(scores(*tiles[k + LEAD]))
        finish(*tile, *ready[k])


def attend(bias, kept, fresh, own_kv, queries):
    rows, width = queries.shape
    heads = width // HD
    step = PAIR if heads % PAIR == 0 else 1
    keys = kept.shape[0] + fresh.shape[0] + rows
    flops = 4 * heads * rows * keys * HD
    bytes_accessed = 2 * (kept.size + fresh.size + own_kv.size + 2 * queries.size) + 4 * bias.size

    def full(shape):
        return pl.BlockSpec(shape, lambda g: (0,) * len(shape))

    return pl.pallas_call(
        attend_kernel,
        grid=(heads // step,),
        in_specs=[
            full(bias.shape),
            full(kept.shape),
            full(fresh.shape),
            full(own_kv.shape),
            pl.BlockSpec((rows, step * HD), lambda g: (0, g)),
        ],
        out_specs=pl.BlockSpec((rows, step * HD), lambda g: (0, g)),
        out_shape=jax.ShapeDtypeStruct(queries.shape, queries.dtype),
        compiler_params=pltpu.CompilerParams(dimension_semantics=("arbitrary",)),
        cost_estimate=pl.CostEstimate(
            flops=flops, bytes_accessed=bytes_accessed, transcendentals=heads * rows * keys
        ),
    )(bias, kept, fresh, own_kv, queries)


def per_device(
    n_seq, n_kvh, queries, own_kv, library, fresh_kv, retrieved, stretch_slot, stretch_len, recompute_pos
):
    per_owner = library.shape[0]
    wanted = lookup(stretch_slot, retrieved[0])
    owner = wanted // per_owner
    local = wanted % per_owner
    limits = lookup(stretch_len, wanted)

    pos_local = recompute_pos[0]
    pair = jnp.arange(pos_local.shape[1], dtype=jnp.int32)
    odd_taken = pos_local - 2 * pair[None, :]
    payload = jnp.concatenate([local[:, None], odd_taken], 1)
    devices = jnp.arange(n_seq, dtype=jnp.int32)
    hits = owner[None, :, None] == devices[:, None, None]
    request = jnp.sum(jnp.where(hits, payload[None], 0), axis=1)
    asked = lax.all_to_all(request, "seq", 0, 0, tiled=True)
    which = asked[:, :1, None]
    odd_given = asked[:, 1:, None]
    halves = library.reshape(per_owner, -1, 2, library.shape[2])
    send = None
    for k in range(per_owner):
        kept = jnp.where(odd_given == 0, halves[k, :, 1][None], halves[k, :, 0][None])
        send = kept if send is None else jnp.where(which == k, kept, send)
    recv = lax.all_to_all(send, "seq", 0, 0, tiled=True)

    me = lax.axis_index("kvh")
    width = own_kv.shape[1]
    tokens = fresh_kv.shape[2]
    fresh_local = fresh_kv[0]
    pieces = [lax.dynamic_slice_in_dim(fresh_local, me * width, width, 2)]
    places = [lax.dynamic_slice_in_dim(pos_local, me * tokens, tokens, 1)]
    for shift in range(1, n_kvh):
        target = lax.rem(me + shift, n_kvh)
        piece = lax.dynamic_slice_in_dim(fresh_local, target * width, width, 2)
        pairs = [(i, (i + shift) % n_kvh) for i in range(n_kvh)]
        pieces.append(lax.ppermute(piece, "kvh", pairs))
        source = lax.rem(me + n_kvh - shift, n_kvh)
        places.append(lax.dynamic_slice_in_dim(pos_local, source * tokens, tokens, 1))
    fresh = jnp.concatenate(pieces, 1)
    pos = jnp.concatenate(places, 1)

    kept_at = 2 * pair[None, :] + 1 - odd_taken
    kept_bias = jnp.where(kept_at < limits[:, None], 0.0, -jnp.inf).astype(jnp.float32)
    slot_of = owner[None, :] == devices[:, None]
    kept_bias = jnp.where(slot_of[:, :, None], kept_bias[None], 0.0).sum(1)
    kept_bias = jnp.where(jnp.any(slot_of, 1)[:, None], kept_bias, -jnp.inf)
    fresh_bias = jnp.where(pos < limits[:, None], 0.0, -jnp.inf).astype(jnp.float32)
    bias = jnp.concatenate([kept_bias.reshape(1, -1), fresh_bias.reshape(1, -1)], 1)
    kept = recv.reshape(-1, recv.shape[2])
    return attend(bias, kept, fresh.reshape(-1, fresh.shape[2]), own_kv, queries)


def solution(mesh):
    placed = (
        P("seq", "kvh"),
        P("seq", "kvh"),
        P("seq", None, "kvh"),
        P("seq", None, "kvh", None),
        P("seq", None),
        P(),
        P(),
        P("seq", None, None),
    )
    body = functools.partial(per_device, mesh.shape["seq"], mesh.shape["kvh"])
    return jax.shard_map(body, mesh=mesh, in_specs=placed, out_specs=P("seq", "kvh"), check_vma=False)
```

```python
import functools

import jax
import jax.numpy as jnp
from jax import lax
from jax.experimental import pallas as pl
from jax.experimental.pallas import tpu as pltpu
from jax.sharding import PartitionSpec as P

HD = 128
CL = 128
TR = 128
PAIR = 4
LEAD = 2


def lookup(table, indices):
    hits = indices[..., None] == jnp.arange(table.shape[0], dtype=jnp.int32)
    return jnp.sum(jnp.where(hits, table, 0), axis=-1)


def early_kernel(bias_ref, fresh_ref, own_ref, q_ref, sa_ref):
    rows = q_ref.shape[0]
    nt = (((1,), (1,)), ((), ()))
    split = fresh_ref.shape[0]
    for g in range(q_ref.shape[1] // HD):
        for t in range(rows // TR):
            qt = q_ref[t * TR:(t + 1) * TR, g * HD:(g + 1) * HD]
            sf = lax.dot_general(qt, fresh_ref[:, :HD], nt, preferred_element_type=jnp.float32)
            sa_ref[g, t * TR:(t + 1) * TR, :split] = sf + bias_ref[...]
            so = lax.dot_general(qt, own_ref[:, :HD], nt, preferred_element_type=jnp.float32)
            row = lax.broadcasted_iota(jnp.int32, so.shape, 0) + t * TR
            col = lax.broadcasted_iota(jnp.int32, so.shape, 1)
            sa_ref[g, t * TR:(t + 1) * TR, split:] = jnp.where(col <= row, so, -jnp.inf)


def attend_kernel(bias_ref, kept_ref, fresh_ref, own_ref, q_ref, sa_ref, out_ref):
    rows = q_ref.shape[0]
    rate = HD ** (-0.5) * 1.4426950408889634
    nt = (((1,), (1,)), ((), ()))
    split = fresh_ref.shape[0]

    def scores(g, t):
        qt = q_ref[t * TR:(t + 1) * TR, g * HD:(g + 1) * HD]
        sk = lax.dot_general(qt, kept_ref[:, :HD], nt, preferred_element_type=jnp.float32)
        return sk + bias_ref[...], sa_ref[g, t * TR:(t + 1) * TR, :]

    def finish(g, t, s1, s2):
        kk = (t + 1) * TR
        top = jnp.maximum(jnp.max(s1, axis=1, keepdims=True), jnp.max(s2, axis=1, keepdims=True))
        e1 = jnp.exp2((s1 - top) * rate)
        e2 = jnp.exp2((s2 - top) * rate)
        inv = 1.0 / (jnp.sum(e1, axis=1, keepdims=True) + jnp.sum(e2, axis=1, keepdims=True))
        w1 = (e1 * inv).astype(jnp.bfloat16)
        w2 = (e2 * inv).astype(jnp.bfloat16)
        mixed = jnp.dot(w1, kept_ref[:, HD:], preferred_element_type=jnp.float32)
        mixed = mixed + jnp.dot(w2[:, :split], fresh_ref[:, HD:], preferred_element_type=jnp.float32)
        mixed = mixed + jnp.dot(w2[:, split:split + kk], own_ref[:kk, HD:], preferred_element_type=jnp.float32)
        out_ref[t * TR:(t + 1) * TR, g * HD:(g + 1) * HD] = mixed.astype(out_ref.dtype)

    tiles = [(g, t) for g in range(q_ref.shape[1] // HD) for t in range(rows // TR)]
    ready = [scores(*tile) for tile in tiles[:LEAD]]
    for k, tile in enumerate(tiles):
        if k + LEAD < len(tiles):
            ready.append(scores(*tiles[k + LEAD]))
        finish(*tile, *ready[k])


def full(shape):
    return pl.BlockSpec(shape, lambda g: (0,) * len(shape))


def early(fresh_bias, fresh, own_kv, queries):
    rows, width = queries.shape
    heads = width // HD
    step = PAIR if heads % PAIR == 0 else 1
    keys = fresh.shape[0] + rows
    block = (step, rows, keys)
    return pl.pallas_call(
        early_kernel,
        grid=(heads // step,),
        in_specs=[
            full(fresh_bias.shape),
            full(fresh.shape),
            full(own_kv.shape),
            pl.BlockSpec((rows, step * HD), lambda g: (0, g)),
        ],
        out_specs=pl.BlockSpec(block, lambda g: (g, 0, 0)),
        out_shape=jax.ShapeDtypeStruct((heads, rows, keys), jnp.float32),
        compiler_params=pltpu.CompilerParams(dimension_semantics=("arbitrary",)),
        cost_estimate=pl.CostEstimate(
            flops=2 * heads * rows * keys * HD,
            bytes_accessed=2 * (fresh.size + own_kv.size + queries.size) + 4 * heads * rows * keys,
            transcendentals=0,
        ),
    )(fresh_bias, fresh, own_kv, queries)


def attend(kept_bias, kept, fresh, own_kv, queries, partial):
    rows, width = queries.shape
    heads = width // HD
    step = PAIR if heads % PAIR == 0 else 1
    keys = kept.shape[0] + fresh.shape[0] + rows
    flops = 2 * heads * rows * (keys + kept.shape[0]) * HD
    bytes_accessed = 2 * (kept.size + fresh.size + own_kv.size + 2 * queries.size) + 4 * partial.size

    return pl.pallas_call(
        attend_kernel,
        grid=(heads // step,),
        in_specs=[
            full(kept_bias.shape),
            full(kept.shape),
            full(fresh.shape),
            full(own_kv.shape),
            pl.BlockSpec((rows, step * HD), lambda g: (0, g)),
            pl.BlockSpec((step,) + partial.shape[1:], lambda g: (g, 0, 0)),
        ],
        out_specs=pl.BlockSpec((rows, step * HD), lambda g: (0, g)),
        out_shape=jax.ShapeDtypeStruct(queries.shape, queries.dtype),
        compiler_params=pltpu.CompilerParams(dimension_semantics=("arbitrary",)),
        cost_estimate=pl.CostEstimate(
            flops=flops, bytes_accessed=bytes_accessed, transcendentals=heads * rows * keys
        ),
    )(kept_bias, kept, fresh, own_kv, queries, partial)


def per_device(
    n_seq, n_kvh, queries, own_kv, library, fresh_kv, retrieved, stretch_slot, stretch_len, recompute_pos
):
    per_owner = library.shape[0]
    wanted = lookup(stretch_slot, retrieved[0])
    owner = wanted // per_owner
    local = wanted % per_owner
    limits = lookup(stretch_len, wanted)

    pos_local = recompute_pos[0]
    pair = jnp.arange(pos_local.shape[1], dtype=jnp.int32)
    odd_taken = pos_local - 2 * pair[None, :]
    payload = jnp.concatenate([local[:, None], odd_taken], 1)
    devices = jnp.arange(n_seq, dtype=jnp.int32)
    hits = owner[None, :, None] == devices[:, None, None]
    request = jnp.sum(jnp.where(hits, payload[None], 0), axis=1)
    asked = lax.all_to_all(request, "seq", 0, 0, tiled=True)
    which = asked[:, :1, None]
    odd_given = asked[:, 1:, None]
    halves = library.reshape(per_owner, -1, 2, library.shape[2])
    send = None
    for k in range(per_owner):
        kept = jnp.where(odd_given == 0, halves[k, :, 1][None], halves[k, :, 0][None])
        send = kept if send is None else jnp.where(which == k, kept, send)
    recv = lax.all_to_all(send, "seq", 0, 0, tiled=True)

    me = lax.axis_index("kvh")
    width = own_kv.shape[1]
    tokens = fresh_kv.shape[2]
    fresh_local = fresh_kv[0]
    pieces = [lax.dynamic_slice_in_dim(fresh_local, me * width, width, 2)]
    places = [lax.dynamic_slice_in_dim(pos_local, me * tokens, tokens, 1)]
    for shift in range(1, n_kvh):
        target = lax.rem(me + shift, n_kvh)
        piece = lax.dynamic_slice_in_dim(fresh_local, target * width, width, 2)
        pairs = [(i, (i + shift) % n_kvh) for i in range(n_kvh)]
        pieces.append(lax.ppermute(piece, "kvh", pairs))
        source = lax.rem(me + n_kvh - shift, n_kvh)
        places.append(lax.dynamic_slice_in_dim(pos_local, source * tokens, tokens, 1))
    fresh = jnp.concatenate(pieces, 1)
    pos = jnp.concatenate(places, 1)

    kept_at = 2 * pair[None, :] + 1 - odd_taken
    kept_bias = jnp.where(kept_at < limits[:, None], 0.0, -jnp.inf).astype(jnp.float32)
    slot_of = owner[None, :] == devices[:, None]
    kept_bias = jnp.where(slot_of[:, :, None], kept_bias[None], 0.0).sum(1)
    kept_bias = jnp.where(jnp.any(slot_of, 1)[:, None], kept_bias, -jnp.inf)
    fresh_bias = jnp.where(pos < limits[:, None], 0.0, -jnp.inf).astype(jnp.float32)
    fresh = fresh.reshape(-1, fresh.shape[2])
    partial = early(fresh_bias.reshape(1, -1), fresh, own_kv, queries)
    kept = recv.reshape(-1, recv.shape[2])
    return attend(kept_bias.reshape(1, -1), kept, fresh, own_kv, queries, partial)


def solution(mesh):
    placed = (
        P("seq", "kvh"),
        P("seq", "kvh"),
        P("seq", None, "kvh"),
        P("seq", None, "kvh", None),
        P("seq", None),
        P(),
        P(),
        P("seq", None, None),
    )
    body = functools.partial(per_device, mesh.shape["seq"], mesh.shape["kvh"])
    return jax.shard_map(body, mesh=mesh, in_specs=placed, out_specs=P("seq", "kvh"), check_vma=False)
```

```python
import functools

import jax
import jax.numpy as jnp
from jax import lax
from jax.experimental import pallas as pl
from jax.experimental.pallas import tpu as pltpu
from jax.sharding import PartitionSpec as P

HD = 128
CL = 128
TR = 128
PAIR = 4
LEAD = 2


def lookup(table, indices):
    hits = indices[..., None] == jnp.arange(table.shape[0], dtype=jnp.int32)
    return jnp.sum(jnp.where(hits, table, 0), axis=-1)


def attend_kernel(bias_ref, kept_ref, fresh_ref, own_ref, q_ref, out_ref):
    rows = q_ref.shape[0]
    rate = HD ** (-0.5) * 1.4426950408889634
    nt = (((1,), (1,)), ((), ()))

    def scores(g, t):
        qt = q_ref[t * TR:(t + 1) * TR, g * HD:(g + 1) * HD]
        sk = lax.dot_general(qt, kept_ref[:, :HD], nt, preferred_element_type=jnp.float32)
        sf = lax.dot_general(qt, fresh_ref[:, :HD], nt, preferred_element_type=jnp.float32)
        s1 = jnp.concatenate([sk, sf], 1) + bias_ref[...]
        kk = (t + 1) * TR
        s2 = lax.dot_general(qt, own_ref[:kk, :HD], nt, preferred_element_type=jnp.float32)
        row = lax.broadcasted_iota(jnp.int32, (TR, kk), 0) + t * TR
        col = lax.broadcasted_iota(jnp.int32, (TR, kk), 1)
        return s1, jnp.where(col <= row, s2, -jnp.inf)

    def finish(g, t, s1, s2):
        kk = (t + 1) * TR
        top = jnp.maximum(jnp.max(s1, axis=1, keepdims=True), jnp.max(s2, axis=1, keepdims=True))
        e1 = jnp.exp2((s1 - top) * rate)
        e2 = jnp.exp2((s2 - top) * rate)
        inv = 1.0 / (jnp.sum(e1, axis=1, keepdims=True) + jnp.sum(e2, axis=1, keepdims=True))
        w1 = (e1 * inv).astype(jnp.bfloat16)
        w2 = (e2 * inv).astype(jnp.bfloat16)
        split = kept_ref.shape[0]
        mixed = jnp.dot(w1[:, :split], kept_ref[:, HD:], preferred_element_type=jnp.float32)
        mixed = mixed + jnp.dot(w1[:, split:], fresh_ref[:, HD:], preferred_element_type=jnp.float32)
        mixed = mixed + jnp.dot(w2, own_ref[:kk, HD:], preferred_element_type=jnp.float32)
        out_ref[t * TR:(t + 1) * TR, g * HD:(g + 1) * HD] = mixed.astype(out_ref.dtype)

    tiles = [(g, t) for g in range(q_ref.shape[1] // HD) for t in range(rows // TR)]
    ready = [scores(*tile) for tile in tiles[:LEAD]]
    for k, tile in enumerate(tiles):
        if k + LEAD < len(tiles):
            ready.append(scores(*tiles[k + LEAD]))
        finish(*tile, *ready[k])


def attend(bias, kept, fresh, own_kv, queries):
    rows, width = queries.shape
    heads = width // HD
    step = PAIR if heads % PAIR == 0 else 1
    keys = kept.shape[0] + fresh.shape[0] + rows
    flops = 4 * heads * rows * keys * HD
    bytes_accessed = 2 * (kept.size + fresh.size + own_kv.size + 2 * queries.size) + 4 * bias.size

    def full(shape):
        return pl.BlockSpec(shape, lambda g: (0,) * len(shape))

    return pl.pallas_call(
        attend_kernel,
        grid=(heads // step,),
        in_specs=[
            full(bias.shape),
            full(kept.shape),
            full(fresh.shape),
            full(own_kv.shape),
            pl.BlockSpec((rows, step * HD), lambda g: (0, g)),
        ],
        out_specs=pl.BlockSpec((rows, step * HD), lambda g: (0, g)),
        out_shape=jax.ShapeDtypeStruct(queries.shape, queries.dtype),
        compiler_params=pltpu.CompilerParams(dimension_semantics=("arbitrary",)),
        cost_estimate=pl.CostEstimate(
            flops=flops, bytes_accessed=bytes_accessed, transcendentals=heads * rows * keys
        ),
    )(bias, kept, fresh, own_kv, queries)


def per_device(
    n_seq, n_kvh, queries, own_kv, library, fresh_kv, retrieved, stretch_slot, stretch_len, recompute_pos
):
    per_owner = library.shape[0]
    wanted = jnp.take(stretch_slot, retrieved[0], mode="clip")
    owner = wanted // per_owner
    limits = jnp.take(stretch_len, wanted, mode="clip")

    pos_local = recompute_pos[0]
    pair = jnp.arange(pos_local.shape[1], dtype=jnp.int32)
    odd_taken = pos_local - 2 * pair[None, :]
    column = jnp.arange(pos_local.shape[1] + 1, dtype=jnp.int32)
    shifted = jnp.pad(pos_local, ((0, 0), (1, 0))) - 2 * column[None, :] + 2
    payload = jnp.where(column[None, :] == 0, (wanted - owner * per_owner)[:, None], shifted)
    devices = jnp.arange(n_seq, dtype=jnp.int32)
    hits = owner[None, :, None] == devices[:, None, None]
    request = jnp.sum(jnp.where(hits, payload[None], 0), axis=1)
    asked = lax.all_to_all(request, "seq", 0, 0, tiled=True)
    which = asked[:, :1, None]
    odd_given = asked[:, 1:, None]
    halves = library.reshape(per_owner, -1, 2, library.shape[2])
    send = None
    for k in range(per_owner):
        kept = jnp.where(odd_given == 0, halves[k, :, 1][None], halves[k, :, 0][None])
        send = kept if send is None else jnp.where(which == k, kept, send)
    recv = lax.all_to_all(send, "seq", 0, 0, tiled=True)

    me = lax.axis_index("kvh")
    width = own_kv.shape[1]
    tokens = fresh_kv.shape[2]
    fresh_local = fresh_kv[0]
    pieces = [lax.dynamic_slice_in_dim(fresh_local, me * width, width, 2)]
    places = [lax.dynamic_slice_in_dim(pos_local, me * tokens, tokens, 1)]
    for shift in range(1, n_kvh):
        target = lax.rem(me + shift, n_kvh)
        piece = lax.dynamic_slice_in_dim(fresh_local, target * width, width, 2)
        pairs = [(i, (i + shift) % n_kvh) for i in range(n_kvh)]
        pieces.append(lax.ppermute(piece, "kvh", pairs))
        source = lax.rem(me + n_kvh - shift, n_kvh)
        places.append(lax.dynamic_slice_in_dim(pos_local, source * tokens, tokens, 1))
    fresh = jnp.concatenate(pieces, 1)
    pos = jnp.concatenate(places, 1)

    kept_at = 2 * pair[None, :] + 1 - odd_taken
    kept_bias = jnp.where(kept_at < limits[:, None], 0.0, -jnp.inf).astype(jnp.float32)
    slot_of = owner[None, :] == devices[:, None]
    kept_bias = jnp.where(slot_of[:, :, None], kept_bias[None], 0.0).sum(1)
    kept_bias = jnp.where(jnp.any(slot_of, 1)[:, None], kept_bias, -jnp.inf)
    fresh_bias = jnp.where(pos < limits[:, None], 0.0, -jnp.inf).astype(jnp.float32)
    bias = jnp.concatenate([kept_bias.reshape(1, -1), fresh_bias.reshape(1, -1)], 1)
    kept = recv.reshape(-1, recv.shape[2])
    return attend(bias, kept, fresh.reshape(-1, fresh.shape[2]), own_kv, queries)


def solution(mesh):
    placed = (
        P("seq", "kvh"),
        P("seq", "kvh"),
        P("seq", None, "kvh"),
        P("seq", None, "kvh", None),
        P("seq", None),
        P(),
        P(),
        P("seq", None, None),
    )
    body = functools.partial(per_device, mesh.shape["seq"], mesh.shape["kvh"])
    return jax.shard_map(body, mesh=mesh, in_specs=placed, out_specs=P("seq", "kvh"), check_vma=False)
```

```python
import functools

import jax
import jax.numpy as jnp
from jax import lax
from jax.experimental import pallas as pl
from jax.experimental.pallas import tpu as pltpu
from jax.sharding import PartitionSpec as P

HD = 128
CL = 128
TR = 128
PAIR = 4
LEAD = 2


def lookup(table, indices):
    hits = indices[..., None] == jnp.arange(table.shape[0], dtype=jnp.int32)
    return jnp.sum(jnp.where(hits, table, 0), axis=-1)


def attend_kernel(bias_ref, kept_ref, fresh_ref, own_ref, q_ref, out_ref):
    rows = q_ref.shape[0]
    rate = HD ** (-0.5) * 1.4426950408889634
    nt = (((1,), (1,)), ((), ()))

    def scores(g, t):
        qt = q_ref[t * TR:(t + 1) * TR, g * HD:(g + 1) * HD]
        sk = lax.dot_general(qt, kept_ref[:, :HD], nt, preferred_element_type=jnp.float32)
        sf = lax.dot_general(qt, fresh_ref[:, :HD], nt, preferred_element_type=jnp.float32)
        s1 = jnp.concatenate([sk, sf], 1) + bias_ref[...]
        kk = (t + 1) * TR
        s2 = lax.dot_general(qt, own_ref[:kk, :HD], nt, preferred_element_type=jnp.float32)
        row = lax.broadcasted_iota(jnp.int32, (TR, kk), 0) + t * TR
        col = lax.broadcasted_iota(jnp.int32, (TR, kk), 1)
        return s1, jnp.where(col <= row, s2, -jnp.inf)

    def finish(g, t, s1, s2):
        kk = (t + 1) * TR
        top = jnp.maximum(jnp.max(s1, axis=1, keepdims=True), jnp.max(s2, axis=1, keepdims=True))
        e1 = jnp.exp2((s1 - top) * rate)
        e2 = jnp.exp2((s2 - top) * rate)
        inv = 1.0 / (jnp.sum(e1, axis=1, keepdims=True) + jnp.sum(e2, axis=1, keepdims=True))
        w1 = (e1 * inv).astype(jnp.bfloat16)
        w2 = (e2 * inv).astype(jnp.bfloat16)
        split = kept_ref.shape[0]
        mixed = jnp.dot(w1[:, :split], kept_ref[:, HD:], preferred_element_type=jnp.float32)
        mixed = mixed + jnp.dot(w1[:, split:], fresh_ref[:, HD:], preferred_element_type=jnp.float32)
        mixed = mixed + jnp.dot(w2, own_ref[:kk, HD:], preferred_element_type=jnp.float32)
        out_ref[t * TR:(t + 1) * TR, g * HD:(g + 1) * HD] = mixed.astype(out_ref.dtype)

    tiles = [(g, t) for g in range(q_ref.shape[1] // HD) for t in range(rows // TR)]
    ready = [scores(*tile) for tile in tiles[:LEAD]]
    for k, tile in enumerate(tiles):
        if k + LEAD < len(tiles):
            ready.append(scores(*tiles[k + LEAD]))
        finish(*tile, *ready[k])


def attend(bias, kept, fresh, own_kv, queries):
    rows, width = queries.shape
    heads = width // HD
    step = PAIR if heads % PAIR == 0 else 1
    keys = kept.shape[0] + fresh.shape[0] + rows
    flops = 4 * heads * rows * keys * HD
    bytes_accessed = 2 * (kept.size + fresh.size + own_kv.size + 2 * queries.size) + 4 * bias.size

    def full(shape):
        return pl.BlockSpec(shape, lambda g: (0,) * len(shape))

    return pl.pallas_call(
        attend_kernel,
        grid=(heads // step,),
        in_specs=[
            full(bias.shape),
            full(kept.shape),
            full(fresh.shape),
            full(own_kv.shape),
            pl.BlockSpec((rows, step * HD), lambda g: (0, g)),
        ],
        out_specs=pl.BlockSpec((rows, step * HD), lambda g: (0, g)),
        out_shape=jax.ShapeDtypeStruct(queries.shape, queries.dtype),
        compiler_params=pltpu.CompilerParams(dimension_semantics=("arbitrary",)),
        cost_estimate=pl.CostEstimate(
            flops=flops, bytes_accessed=bytes_accessed, transcendentals=heads * rows * keys
        ),
    )(bias, kept, fresh, own_kv, queries)


def two_stage(table, n):
    inner = max(d for d in range(1, n + 1) if n % d == 0 and d * d <= n)
    outer = n // inner
    rest = table.shape[1:]
    near = [[a * inner + b for b in range(inner)] for a in range(outer)]
    far = [[a * inner + b for a in range(outer)] for b in range(inner)]
    table = table.reshape((outer, inner) + rest)
    table = lax.all_to_all(table, "seq", 1, 1, axis_index_groups=near, tiled=True)
    table = lax.all_to_all(table, "seq", 0, 0, axis_index_groups=far, tiled=True)
    return table.reshape((n,) + rest)


def per_device(
    n_seq, n_kvh, queries, own_kv, library, fresh_kv, retrieved, stretch_slot, stretch_len, recompute_pos
):
    per_owner = library.shape[0]
    wanted = lookup(stretch_slot, retrieved[0])
    owner = wanted // per_owner
    local = wanted % per_owner
    limits = lookup(stretch_len, wanted)

    pos_local = recompute_pos[0]
    pair = jnp.arange(pos_local.shape[1], dtype=jnp.int32)
    odd_taken = pos_local - 2 * pair[None, :]
    payload = jnp.concatenate([local[:, None], odd_taken], 1)
    devices = jnp.arange(n_seq, dtype=jnp.int32)
    hits = owner[None, :, None] == devices[:, None, None]
    request = jnp.sum(jnp.where(hits, payload[None], 0), axis=1)
    asked = two_stage(request, n_seq)
    which = asked[:, :1, None]
    odd_given = asked[:, 1:, None]
    halves = library.reshape(per_owner, -1, 2, library.shape[2])
    send = None
    for k in range(per_owner):
        kept = jnp.where(odd_given == 0, halves[k, :, 1][None], halves[k, :, 0][None])
        send = kept if send is None else jnp.where(which == k, kept, send)
    recv = lax.all_to_all(send, "seq", 0, 0, tiled=True)

    me = lax.axis_index("kvh")
    width = own_kv.shape[1]
    tokens = fresh_kv.shape[2]
    fresh_local = fresh_kv[0]
    pieces = [lax.dynamic_slice_in_dim(fresh_local, me * width, width, 2)]
    places = [lax.dynamic_slice_in_dim(pos_local, me * tokens, tokens, 1)]
    for shift in range(1, n_kvh):
        target = lax.rem(me + shift, n_kvh)
        piece = lax.dynamic_slice_in_dim(fresh_local, target * width, width, 2)
        pairs = [(i, (i + shift) % n_kvh) for i in range(n_kvh)]
        pieces.append(lax.ppermute(piece, "kvh", pairs))
        source = lax.rem(me + n_kvh - shift, n_kvh)
        places.append(lax.dynamic_slice_in_dim(pos_local, source * tokens, tokens, 1))
    fresh = jnp.concatenate(pieces, 1)
    pos = jnp.concatenate(places, 1)

    kept_at = 2 * pair[None, :] + 1 - odd_taken
    kept_bias = jnp.where(kept_at < limits[:, None], 0.0, -jnp.inf).astype(jnp.float32)
    slot_of = owner[None, :] == devices[:, None]
    kept_bias = jnp.where(slot_of[:, :, None], kept_bias[None], 0.0).sum(1)
    kept_bias = jnp.where(jnp.any(slot_of, 1)[:, None], kept_bias, -jnp.inf)
    fresh_bias = jnp.where(pos < limits[:, None], 0.0, -jnp.inf).astype(jnp.float32)
    bias = jnp.concatenate([kept_bias.reshape(1, -1), fresh_bias.reshape(1, -1)], 1)
    kept = recv.reshape(-1, recv.shape[2])
    return attend(bias, kept, fresh.reshape(-1, fresh.shape[2]), own_kv, queries)


def solution(mesh):
    placed = (
        P("seq", "kvh"),
        P("seq", "kvh"),
        P("seq", None, "kvh"),
        P("seq", None, "kvh", None),
        P("seq", None),
        P(),
        P(),
        P("seq", None, None),
    )
    body = functools.partial(per_device, mesh.shape["seq"], mesh.shape["kvh"])
    return jax.shard_map(body, mesh=mesh, in_specs=placed, out_specs=P("seq", "kvh"), check_vma=False)
```

```python
import functools

import jax
import jax.numpy as jnp
from jax import lax
from jax.experimental import pallas as pl
from jax.experimental.pallas import tpu as pltpu
from jax.sharding import PartitionSpec as P

HD = 128
CL = 128
TR = 128
PAIR = 8
LEAD = 2


def lookup(table, indices):
    hits = indices[..., None] == jnp.arange(table.shape[0], dtype=jnp.int32)
    return jnp.sum(jnp.where(hits, table, 0), axis=-1)


def attend_kernel(bias_ref, kept_ref, fresh_ref, own_ref, q_ref, out_ref):
    rows = q_ref.shape[0]
    rate = HD ** (-0.5) * 1.4426950408889634
    nt = (((1,), (1,)), ((), ()))

    def scores(g, t):
        qt = q_ref[t * TR:(t + 1) * TR, g * HD:(g + 1) * HD]
        sk = lax.dot_general(qt, kept_ref[:, :HD], nt, preferred_element_type=jnp.float32)
        sf = lax.dot_general(qt, fresh_ref[:, :HD], nt, preferred_element_type=jnp.float32)
        s1 = jnp.concatenate([sk, sf], 1) + bias_ref[...]
        kk = (t + 1) * TR
        s2 = lax.dot_general(qt, own_ref[:kk, :HD], nt, preferred_element_type=jnp.float32)
        row = lax.broadcasted_iota(jnp.int32, (TR, kk), 0) + t * TR
        col = lax.broadcasted_iota(jnp.int32, (TR, kk), 1)
        return s1, jnp.where(col <= row, s2, -jnp.inf)

    def finish(g, t, s1, s2):
        kk = (t + 1) * TR
        top = jnp.maximum(jnp.max(s1, axis=1, keepdims=True), jnp.max(s2, axis=1, keepdims=True))
        e1 = jnp.exp2((s1 - top) * rate)
        e2 = jnp.exp2((s2 - top) * rate)
        inv = 1.0 / (jnp.sum(e1, axis=1, keepdims=True) + jnp.sum(e2, axis=1, keepdims=True))
        w1 = (e1 * inv).astype(jnp.bfloat16)
        w2 = (e2 * inv).astype(jnp.bfloat16)
        split = kept_ref.shape[0]
        mixed = jnp.dot(w1[:, :split], kept_ref[:, HD:], preferred_element_type=jnp.float32)
        mixed = mixed + jnp.dot(w1[:, split:], fresh_ref[:, HD:], preferred_element_type=jnp.float32)
        mixed = mixed + jnp.dot(w2, own_ref[:kk, HD:], preferred_element_type=jnp.float32)
        out_ref[t * TR:(t + 1) * TR, g * HD:(g + 1) * HD] = mixed.astype(out_ref.dtype)

    tiles = [(g, t) for g in range(q_ref.shape[1] // HD) for t in range(rows // TR)]
    ready = [scores(*tile) for tile in tiles[:LEAD]]
    for k, tile in enumerate(tiles):
        if k + LEAD < len(tiles):
            ready.append(scores(*tiles[k + LEAD]))
        finish(*tile, *ready[k])


def attend(bias, kept, fresh, own_kv, queries):
    rows, width = queries.shape
    heads = width // HD
    step = PAIR if heads % PAIR == 0 else 1
    keys = kept.shape[0] + fresh.shape[0] + rows
    flops = 4 * heads * rows * keys * HD
    bytes_accessed = 2 * (kept.size + fresh.size + own_kv.size + 2 * queries.size) + 4 * bias.size

    def full(shape):
        return pl.BlockSpec(shape, lambda g: (0,) * len(shape))

    return pl.pallas_call(
        attend_kernel,
        grid=(heads // step,),
        in_specs=[
            full(bias.shape),
            full(kept.shape),
            full(fresh.shape),
            full(own_kv.shape),
            pl.BlockSpec((rows, step * HD), lambda g: (0, g)),
        ],
        out_specs=pl.BlockSpec((rows, step * HD), lambda g: (0, g)),
        out_shape=jax.ShapeDtypeStruct(queries.shape, queries.dtype),
        compiler_params=pltpu.CompilerParams(dimension_semantics=("arbitrary",)),
        cost_estimate=pl.CostEstimate(
            flops=flops, bytes_accessed=bytes_accessed, transcendentals=heads * rows * keys
        ),
    )(bias, kept, fresh, own_kv, queries)


def per_device(
    n_seq, n_kvh, queries, own_kv, library, fresh_kv, retrieved, stretch_slot, stretch_len, recompute_pos
):
    per_owner = library.shape[0]
    wanted = lookup(stretch_slot, retrieved[0])
    owner = wanted // per_owner
    local = wanted % per_owner
    limits = lookup(stretch_len, wanted)

    pos_local = recompute_pos[0]
    pair = jnp.arange(pos_local.shape[1], dtype=jnp.int32)
    odd_taken = pos_local - 2 * pair[None, :]
    payload = jnp.concatenate([local[:, None], odd_taken], 1)
    devices = jnp.arange(n_seq, dtype=jnp.int32)
    hits = owner[None, :, None] == devices[:, None, None]
    request = jnp.sum(jnp.where(hits, payload[None], 0), axis=1)
    asked = lax.all_to_all(request, "seq", 0, 0, tiled=True)
    which = asked[:, :1, None]
    odd_given = asked[:, 1:, None]
    halves = library.reshape(per_owner, -1, 2, library.shape[2])
    send = None
    for k in range(per_owner):
        kept = jnp.where(odd_given == 0, halves[k, :, 1][None], halves[k, :, 0][None])
        send = kept if send is None else jnp.where(which == k, kept, send)
    recv = lax.all_to_all(send, "seq", 0, 0, tiled=True)

    me = lax.axis_index("kvh")
    width = own_kv.shape[1]
    tokens = fresh_kv.shape[2]
    fresh_local = fresh_kv[0]
    pieces = [lax.dynamic_slice_in_dim(fresh_local, me * width, width, 2)]
    places = [lax.dynamic_slice_in_dim(pos_local, me * tokens, tokens, 1)]
    for shift in range(1, n_kvh):
        target = lax.rem(me + shift, n_kvh)
        piece = lax.dynamic_slice_in_dim(fresh_local, target * width, width, 2)
        pairs = [(i, (i + shift) % n_kvh) for i in range(n_kvh)]
        pieces.append(lax.ppermute(piece, "kvh", pairs))
        source = lax.rem(me + n_kvh - shift, n_kvh)
        places.append(lax.dynamic_slice_in_dim(pos_local, source * tokens, tokens, 1))
    fresh = jnp.concatenate(pieces, 1)
    pos = jnp.concatenate(places, 1)

    kept_at = 2 * pair[None, :] + 1 - odd_taken
    kept_bias = jnp.where(kept_at < limits[:, None], 0.0, -jnp.inf).astype(jnp.float32)
    slot_of = owner[None, :] == devices[:, None]
    kept_bias = jnp.where(slot_of[:, :, None], kept_bias[None], 0.0).sum(1)
    kept_bias = jnp.where(jnp.any(slot_of, 1)[:, None], kept_bias, -jnp.inf)
    fresh_bias = jnp.where(pos < limits[:, None], 0.0, -jnp.inf).astype(jnp.float32)
    bias = jnp.concatenate([kept_bias.reshape(1, -1), fresh_bias.reshape(1, -1)], 1)
    kept = recv.reshape(-1, recv.shape[2])
    return attend(bias, kept, fresh.reshape(-1, fresh.shape[2]), own_kv, queries)


def solution(mesh):
    placed = (
        P("seq", "kvh"),
        P("seq", "kvh"),
        P("seq", None, "kvh"),
        P("seq", None, "kvh", None),
        P("seq", None),
        P(),
        P(),
        P("seq", None, None),
    )
    body = functools.partial(per_device, mesh.shape["seq"], mesh.shape["kvh"])
    return jax.shard_map(body, mesh=mesh, in_specs=placed, out_specs=P("seq", "kvh"), check_vma=False)
```

```python
import functools

import jax
import jax.numpy as jnp
from jax import lax
from jax.experimental import pallas as pl
from jax.experimental.pallas import tpu as pltpu
from jax.sharding import PartitionSpec as P

HD = 128
CL = 128
TR = 128
PAIR = 4
LEAD = 2


def lookup(table, indices):
    hits = indices[..., None] == jnp.arange(table.shape[0], dtype=jnp.int32)
    return jnp.sum(jnp.where(hits, table, 0), axis=-1)


def attend_kernel(bias_ref, kept_ref, fresh_ref, own_ref, q_ref, out_ref):
    rows = q_ref.shape[0]
    rate = HD ** (-0.5) * 1.4426950408889634
    nt = (((1,), (1,)), ((), ()))

    def scores(g, t):
        qt = q_ref[t * TR:(t + 1) * TR, g * HD:(g + 1) * HD]
        sk = lax.dot_general(qt, kept_ref[:, :HD], nt, preferred_element_type=jnp.float32)
        sf = lax.dot_general(qt, fresh_ref[:, :HD], nt, preferred_element_type=jnp.float32)
        s1 = jnp.concatenate([sk, sf], 1) + bias_ref[...]
        kk = (t + 1) * TR
        s2 = lax.dot_general(qt, own_ref[:kk, :HD], nt, preferred_element_type=jnp.float32)
        row = lax.broadcasted_iota(jnp.int32, (TR, kk), 0) + t * TR
        col = lax.broadcasted_iota(jnp.int32, (TR, kk), 1)
        return s1, jnp.where(col <= row, s2, -jnp.inf)

    def finish(g, t, s1, s2):
        kk = (t + 1) * TR
        top = jnp.maximum(jnp.max(s1, axis=1, keepdims=True), jnp.max(s2, axis=1, keepdims=True))
        e1 = jnp.exp2((s1 - top) * rate)
        e2 = jnp.exp2((s2 - top) * rate)
        inv = 1.0 / (jnp.sum(e1, axis=1, keepdims=True) + jnp.sum(e2, axis=1, keepdims=True))
        w1 = (e1 * inv).astype(jnp.bfloat16)
        w2 = (e2 * inv).astype(jnp.bfloat16)
        split = kept_ref.shape[0]
        mixed = jnp.dot(w1[:, :split], kept_ref[:, HD:], preferred_element_type=jnp.float32)
        mixed = mixed + jnp.dot(w1[:, split:], fresh_ref[:, HD:], preferred_element_type=jnp.float32)
        mixed = mixed + jnp.dot(w2, own_ref[:kk, HD:], preferred_element_type=jnp.float32)
        out_ref[t * TR:(t + 1) * TR, g * HD:(g + 1) * HD] = mixed.astype(out_ref.dtype)

    tiles = [(g, t) for g in range(q_ref.shape[1] // HD) for t in range(rows // TR)]
    ready = [scores(*tile) for tile in tiles[:LEAD]]
    for k, tile in enumerate(tiles):
        if k + LEAD < len(tiles):
            ready.append(scores(*tiles[k + LEAD]))
        finish(*tile, *ready[k])


def attend(bias, kept, fresh, own_kv, queries):
    rows, width = queries.shape
    heads = width // HD
    step = PAIR if heads % PAIR == 0 else 1
    keys = kept.shape[0] + fresh.shape[0] + rows
    flops = 4 * heads * rows * keys * HD
    bytes_accessed = 2 * (kept.size + fresh.size + own_kv.size + 2 * queries.size) + 4 * bias.size

    def full(shape):
        return pl.BlockSpec(shape, lambda g: (0,) * len(shape))

    return pl.pallas_call(
        attend_kernel,
        grid=(heads // step,),
        in_specs=[
            full(bias.shape),
            full(kept.shape),
            full(fresh.shape),
            full(own_kv.shape),
            pl.BlockSpec((rows, step * HD), lambda g: (0, g)),
        ],
        out_specs=pl.BlockSpec((rows, step * HD), lambda g: (0, g)),
        out_shape=jax.ShapeDtypeStruct(queries.shape, queries.dtype),
        compiler_params=pltpu.CompilerParams(dimension_semantics=("arbitrary",)),
        cost_estimate=pl.CostEstimate(
            flops=flops, bytes_accessed=bytes_accessed, transcendentals=heads * rows * keys
        ),
    )(bias, kept, fresh, own_kv, queries)


def per_device(
    n_seq, n_kvh, queries, own_kv, library, fresh_kv, retrieved, stretch_slot, stretch_len, recompute_pos
):
    per_owner = library.shape[0]
    wanted = lookup(stretch_slot, retrieved[0])
    owner = wanted // per_owner
    local = wanted % per_owner
    limits = lookup(stretch_len, wanted)

    pos_local = recompute_pos[0]
    pair = jnp.arange(pos_local.shape[1], dtype=jnp.int32)
    odd_taken = pos_local - 2 * pair[None, :]
    payload = jnp.concatenate([local[:, None], odd_taken], 1)
    devices = jnp.arange(n_seq, dtype=jnp.int32)
    hits = owner[None, :, None] == devices[:, None, None]
    request = jnp.sum(jnp.where(hits, payload[None], 0), axis=1)
    width_asked = request.shape[1]
    request = jnp.pad(request, ((0, 0), (0, 1024 - width_asked))).reshape(n_seq, 8, 128)
    asked = lax.all_to_all(request, "seq", 0, 0, tiled=True)
    asked = asked.reshape(n_seq, 1024)[:, :width_asked]
    which = asked[:, :1, None]
    odd_given = asked[:, 1:, None]
    halves = library.reshape(per_owner, -1, 2, library.shape[2])
    send = None
    for k in range(per_owner):
        kept = jnp.where(odd_given == 0, halves[k, :, 1][None], halves[k, :, 0][None])
        send = kept if send is None else jnp.where(which == k, kept, send)
    recv = lax.all_to_all(send, "seq", 0, 0, tiled=True)

    me = lax.axis_index("kvh")
    width = own_kv.shape[1]
    tokens = fresh_kv.shape[2]
    fresh_local = fresh_kv[0]
    pieces = [lax.dynamic_slice_in_dim(fresh_local, me * width, width, 2)]
    places = [lax.dynamic_slice_in_dim(pos_local, me * tokens, tokens, 1)]
    for shift in range(1, n_kvh):
        target = lax.rem(me + shift, n_kvh)
        piece = lax.dynamic_slice_in_dim(fresh_local, target * width, width, 2)
        pairs = [(i, (i + shift) % n_kvh) for i in range(n_kvh)]
        pieces.append(lax.ppermute(piece, "kvh", pairs))
        source = lax.rem(me + n_kvh - shift, n_kvh)
        places.append(lax.dynamic_slice_in_dim(pos_local, source * tokens, tokens, 1))
    fresh = jnp.concatenate(pieces, 1)
    pos = jnp.concatenate(places, 1)

    kept_at = 2 * pair[None, :] + 1 - odd_taken
    kept_bias = jnp.where(kept_at < limits[:, None], 0.0, -jnp.inf).astype(jnp.float32)
    slot_of = owner[None, :] == devices[:, None]
    kept_bias = jnp.where(slot_of[:, :, None], kept_bias[None], 0.0).sum(1)
    kept_bias = jnp.where(jnp.any(slot_of, 1)[:, None], kept_bias, -jnp.inf)
    fresh_bias = jnp.where(pos < limits[:, None], 0.0, -jnp.inf).astype(jnp.float32)
    bias = jnp.concatenate([kept_bias.reshape(1, -1), fresh_bias.reshape(1, -1)], 1)
    kept = recv.reshape(-1, recv.shape[2])
    return attend(bias, kept, fresh.reshape(-1, fresh.shape[2]), own_kv, queries)


def solution(mesh):
    placed = (
        P("seq", "kvh"),
        P("seq", "kvh"),
        P("seq", None, "kvh"),
        P("seq", None, "kvh", None),
        P("seq", None),
        P(),
        P(),
        P("seq", None, None),
    )
    body = functools.partial(per_device, mesh.shape["seq"], mesh.shape["kvh"])
    return jax.shard_map(body, mesh=mesh, in_specs=placed, out_specs=P("seq", "kvh"), check_vma=False)
```

```python
import functools

import jax
import jax.numpy as jnp
from jax import lax
from jax.experimental import pallas as pl
from jax.experimental.pallas import tpu as pltpu
from jax.sharding import PartitionSpec as P

HD = 128
CL = 128
TR = 128
PAIR = 4
LEAD = 2


def lookup(table, indices):
    hits = indices[..., None] == jnp.arange(table.shape[0], dtype=jnp.int32)
    return jnp.sum(jnp.where(hits, table, 0), axis=-1)


def attend_kernel(bias_ref, kept_ref, fresh_ref, own_ref, q_ref, out_ref):
    rows = q_ref.shape[0]
    rate = HD ** (-0.5) * 1.4426950408889634
    nt = (((1,), (1,)), ((), ()))

    def scores(g, t):
        qt = q_ref[t * TR:(t + 1) * TR, g * HD:(g + 1) * HD]
        sk = lax.dot_general(qt, kept_ref[:, :HD], nt, preferred_element_type=jnp.float32)
        sf = lax.dot_general(qt, fresh_ref[:, :HD], nt, preferred_element_type=jnp.float32)
        s1 = jnp.concatenate([sk, sf], 1) + bias_ref[...]
        kk = (t + 1) * TR
        s2 = lax.dot_general(qt, own_ref[:kk, :HD], nt, preferred_element_type=jnp.float32)
        row = lax.broadcasted_iota(jnp.int32, (TR, kk), 0) + t * TR
        col = lax.broadcasted_iota(jnp.int32, (TR, kk), 1)
        return s1, jnp.where(col <= row, s2, -jnp.inf)

    def finish(g, t, s1, s2):
        kk = (t + 1) * TR
        top = jnp.maximum(jnp.max(s1, axis=1, keepdims=True), jnp.max(s2, axis=1, keepdims=True))
        e1 = jnp.exp2((s1 - top) * rate)
        e2 = jnp.exp2((s2 - top) * rate)
        inv = 1.0 / (jnp.sum(e1, axis=1, keepdims=True) + jnp.sum(e2, axis=1, keepdims=True))
        w1 = (e1 * inv).astype(jnp.bfloat16)
        w2 = (e2 * inv).astype(jnp.bfloat16)
        split = kept_ref.shape[0]
        mixed = jnp.dot(w1[:, :split], kept_ref[:, HD:], preferred_element_type=jnp.float32)
        mixed = mixed + jnp.dot(w1[:, split:], fresh_ref[:, HD:], preferred_element_type=jnp.float32)
        mixed = mixed + jnp.dot(w2, own_ref[:kk, HD:], preferred_element_type=jnp.float32)
        out_ref[t * TR:(t + 1) * TR, g * HD:(g + 1) * HD] = mixed.astype(out_ref.dtype)

    tiles = [(g, t) for g in range(q_ref.shape[1] // HD) for t in range(rows // TR)]
    ready = [scores(*tile) for tile in tiles[:LEAD]]
    for k, tile in enumerate(tiles):
        if k + LEAD < len(tiles):
            ready.append(scores(*tiles[k + LEAD]))
        finish(*tile, *ready[k])


def attend(bias, kept, fresh, own_kv, queries):
    rows, width = queries.shape
    heads = width // HD
    step = PAIR if heads % PAIR == 0 else 1
    keys = kept.shape[0] + fresh.shape[0] + rows
    flops = 4 * heads * rows * keys * HD
    bytes_accessed = 2 * (kept.size + fresh.size + own_kv.size + 2 * queries.size) + 4 * bias.size

    def full(shape):
        return pl.BlockSpec(shape, lambda g: (0,) * len(shape))

    return pl.pallas_call(
        attend_kernel,
        grid=(heads // step,),
        in_specs=[
            full(bias.shape),
            full(kept.shape),
            full(fresh.shape),
            full(own_kv.shape),
            pl.BlockSpec((rows, step * HD), lambda g: (0, g)),
        ],
        out_specs=pl.BlockSpec((rows, step * HD), lambda g: (0, g)),
        out_shape=jax.ShapeDtypeStruct(queries.shape, queries.dtype),
        compiler_params=pltpu.CompilerParams(dimension_semantics=("arbitrary",)),
        cost_estimate=pl.CostEstimate(
            flops=flops, bytes_accessed=bytes_accessed, transcendentals=heads * rows * keys
        ),
    )(bias, kept, fresh, own_kv, queries)


def per_device(
    n_seq, n_kvh, queries, own_kv, library, fresh_kv, retrieved, stretch_slot, stretch_len, recompute_pos
):
    per_owner = library.shape[0]
    wanted = lookup(stretch_slot, retrieved[0])
    owner = wanted // per_owner
    local = wanted % per_owner
    limits = lookup(stretch_len, wanted)

    pos_local = recompute_pos[0]
    pair = jnp.arange(pos_local.shape[1], dtype=jnp.int32)
    odd_taken = pos_local - 2 * pair[None, :]
    payload = jnp.concatenate([local[:, None], odd_taken], 1)
    devices = jnp.arange(n_seq, dtype=jnp.int32)
    hits = owner[None, :, None] == devices[:, None, None]
    request = jnp.sum(jnp.where(hits, payload[None], 0), axis=1)
    asked = lax.all_to_all(request, "seq", 0, 0, tiled=True)
    which = asked[:, :1, None]
    odd_given = asked[:, 1:, None]
    halves = jnp.swapaxes(library.reshape(per_owner, -1, 2, library.shape[2]), 1, 2)
    send = None
    for k in range(per_owner):
        kept = jnp.where(odd_given == 0, halves[k, 1][None], halves[k, 0][None])
        send = kept if send is None else jnp.where(which == k, kept, send)
    recv = lax.all_to_all(send, "seq", 0, 0, tiled=True)

    me = lax.axis_index("kvh")
    width = own_kv.shape[1]
    tokens = fresh_kv.shape[2]
    fresh_local = fresh_kv[0]
    pieces = [lax.dynamic_slice_in_dim(fresh_local, me * width, width, 2)]
    places = [lax.dynamic_slice_in_dim(pos_local, me * tokens, tokens, 1)]
    for shift in range(1, n_kvh):
        target = lax.rem(me + shift, n_kvh)
        piece = lax.dynamic_slice_in_dim(fresh_local, target * width, width, 2)
        pairs = [(i, (i + shift) % n_kvh) for i in range(n_kvh)]
        pieces.append(lax.ppermute(piece, "kvh", pairs))
        source = lax.rem(me + n_kvh - shift, n_kvh)
        places.append(lax.dynamic_slice_in_dim(pos_local, source * tokens, tokens, 1))
    fresh = jnp.concatenate(pieces, 1)
    pos = jnp.concatenate(places, 1)

    kept_at = 2 * pair[None, :] + 1 - odd_taken
    kept_bias = jnp.where(kept_at < limits[:, None], 0.0, -jnp.inf).astype(jnp.float32)
    slot_of = owner[None, :] == devices[:, None]
    kept_bias = jnp.where(slot_of[:, :, None], kept_bias[None], 0.0).sum(1)
    kept_bias = jnp.where(jnp.any(slot_of, 1)[:, None], kept_bias, -jnp.inf)
    fresh_bias = jnp.where(pos < limits[:, None], 0.0, -jnp.inf).astype(jnp.float32)
    bias = jnp.concatenate([kept_bias.reshape(1, -1), fresh_bias.reshape(1, -1)], 1)
    kept = recv.reshape(-1, recv.shape[2])
    return attend(bias, kept, fresh.reshape(-1, fresh.shape[2]), own_kv, queries)


def solution(mesh):
    placed = (
        P("seq", "kvh"),
        P("seq", "kvh"),
        P("seq", None, "kvh"),
        P("seq", None, "kvh", None),
        P("seq", None),
        P(),
        P(),
        P("seq", None, None),
    )
    body = functools.partial(per_device, mesh.shape["seq"], mesh.shape["kvh"])
    return jax.shard_map(body, mesh=mesh, in_specs=placed, out_specs=P("seq", "kvh"), check_vma=False)
```
